32 devices in a mesh: snp: 8 (over z, y), samp: 4 (over x, core).
Axes of the slice: x: 2, y: 2, z: 4, core: 2. Of those that a mesh axis runs over, the one named last changes fastest.
Arguments:
- genotypes: bfloat16 [1536, 5120], P('samp', 'snp'), may hold values from -0.076171875 to 0.076171875
- responses: float32 [3072, 1536], P('snp', 'samp'), may hold values from -6 to 6
- weights: float32 [1024, 64, 128], P('snp'), may hold values from -6 to 6
- pattern: int32 [1024, 2], P('snp'), may hold values from 0 to 45, as said below
- entry_count: int32 [8], P('snp'), may hold values from 64 to 128, as said below
- tile_slot: int32 [46], replicated, may hold values from 0 to 47, as said below
- penalty: float32 [46], replicated, may hold values from 0.5 to 5
Outputs:
- new_weights: float32 [1024, 64, 128], P('snp')
The draws below stay inside these ranges and needn't reach their ends.
Inputs may be any that keep to these rules, and one draw needn't show every extreme that they name: `pattern`: column 0 is a block below 5, column 1 a tile below 46; within one segment's 128 rows no (block, tile) pair repeats. `entry_count`: some segment has all 128 entries live. `tile_slot`: distinct slots.
All inputs are finite; a program needn't handle non-finite values.
Results may differ from the reference program's by a relative error of at most 0.0032.
Values may be sent and summed in bfloat16 or wider, within the bound.
No kernel may reach another device: no remote copies, remote signals or barrier semaphores. Data moves between devices by JAX's collectives and lax.ppermute only.
A program may use at most 128 MiB of HBM per device.

```python
import math
import jax
import jax.numpy as jnp
from jax import lax

PT = 64
PTILES = 46
SB = 128
NBLK = 5
SNPS = 5120
NSAMP = 1536
NE = 128
SLOTS = 48
ITERS = 2
N_SNP = 8


def draw_pattern(key, part):
    pairs = NBLK * PTILES
    keys = jax.random.split(jax.random.fold_in(key, 11), 3)
    center = jax.random.randint(keys[0], (N_SNP, 1), 0, PTILES)
    ident = jnp.arange(pairs, dtype=jnp.int32)
    tile_ids = ident % PTILES
    apart = jnp.abs(tile_ids[None, :] - center)
    apart = jnp.minimum(apart, PTILES - apart)
    coin = jax.random.randint(keys[1], (N_SNP, pairs), 0, 2)
    rough = jax.random.randint(keys[2], (N_SNP, pairs), 0, 1 << 20)
    score = (rough + jnp.where(apart <= 3, coin, 0) * (1 << 20)) * 512 + ident[None, :]
    _, picked = lax.top_k(score, NE)
    both = jnp.stack([picked // PTILES, picked % PTILES], axis=-1)
    return both.reshape(N_SNP * NE, 2).astype(jnp.int32)


def draw_entry_count(key, part):
    keys = jax.random.split(jax.random.fold_in(key, 23), 2)
    counts = jax.random.randint(keys[0], (N_SNP,), NE // 2, NE + 1)
    fullest = jax.random.randint(keys[1], (), 0, N_SNP)
    return jnp.where(jnp.arange(N_SNP) == fullest, NE, counts).astype(jnp.int32)


def draw_tile_slot(key, part):
    order = jax.random.permutation(jax.random.fold_in(key, 37), SLOTS)
    return order[:PTILES].astype(jnp.int32)


def levels(own_key, extent, cuts, smallest, top_value):
    factor_of, own = 1.0, jax.random.fold_in(own_key, 6)
    for axis_at, shards_of in cuts:
        steps = jnp.exp(jax.random.uniform(jax.random.fold_in(own, axis_at), (shards_of,), jnp.float32, smallest / len(cuts), top_value / len(cuts)))
        factor_of = factor_of * jnp.repeat(steps, extent[axis_at] // shards_of).reshape([-1 if axis == axis_at else 1 for axis in range(len(extent))])
    return factor_of


def noise(key, extent, spread, limit, shards=(), kind=jnp.bfloat16):
    drawn = jax.random.normal(key, extent, jnp.float32) * spread
    if len(shards) > 0:
        drawn = levels(key, extent, shards, -0.22, 0.18) * drawn
    return jnp.clip(drawn, min=-limit, max=limit).astype(kind)


def setup_inputs(seed: int = 0) -> dict:
    splits = jax.random.split(jax.random.key(seed), 8)
    genotypes = noise(splits[0], (NSAMP, SNPS), (0.5 / NSAMP ** 0.5), 0.076171875, ((0, 4), (1, 8)))
    responses = noise(splits[1], (SLOTS * PT, NSAMP), 1.0, 6.0, ((0, 8), (1, 4)), jnp.float32)
    weights = noise(splits[2], (N_SNP * NE, PT, SB), 1.0, 6.0, ((0, 8),), jnp.float32)
    pattern = draw_pattern(jax.random.fold_in(splits[7], 71), 0)
    entry_count = draw_entry_count(jax.random.fold_in(splits[7], 71), 0)
    tile_slot = draw_tile_slot(jax.random.fold_in(splits[7], 71), 0)
    penalty = jnp.clip(jnp.exp(jax.random.uniform(splits[6], (PTILES,), jnp.float32, math.log(0.5), math.log(5.0))), 0.5, 5.0)
    return {"genotypes": genotypes, "responses": responses, "weights": weights, "pattern": pattern, "entry_count": entry_count, "tile_slot": tile_slot, "penalty": penalty}


step_scale = 0.3


def reference(genotypes, responses, weights, pattern, entry_count, tile_slot, penalty):
    tiled = weights.reshape(N_SNP, NE, PT, SB)
    layout = pattern.reshape(N_SNP, NE, 2)
    active = jnp.arange(NE, dtype=jnp.int32)[None, :] < entry_count[:, None]
    slot_ids = tile_slot[layout[:, :, 1]].astype(jnp.int32)
    cutoff = step_scale * penalty[layout[:, :, 1]][:, :, None, None]
    columns = genotypes.reshape(NSAMP, N_SNP, NBLK, SB).transpose(1, 0, 2, 3)
    current = jnp.where(active[:, :, None, None], tiled, jnp.float32(0.0))
    targets = responses.reshape(SLOTS, PT, NSAMP)
    for sweep in range(ITERS):
        weight_bf = current.astype(jnp.bfloat16)

        def predict(summed, segment):
            geno_seg, weight_seg, layout_seg, slot_seg = segment
            chosen = geno_seg[:, layout_seg[:, 0], :].astype(jnp.float32)
            products = jnp.einsum("sek,epk->eps", chosen, weight_seg.astype(jnp.float32))
            partial_value = jnp.zeros((SLOTS, PT, NSAMP), jnp.float32).at[slot_seg].add(products)
            partial_value = lax.optimization_barrier(partial_value.astype(jnp.bfloat16)).astype(jnp.float32)
            return summed + partial_value, None

        summed, _ = lax.scan(predict, jnp.zeros((SLOTS, PT, NSAMP), jnp.float32),
                             (columns, weight_bf, layout, slot_ids))
        residual = (targets - summed).astype(jnp.bfloat16)

        def gradient_seg(unused, segment):
            geno_seg, layout_seg, slot_seg = segment
            chosen = geno_seg[:, layout_seg[:, 0], :].astype(jnp.float32)
            picked = residual[slot_seg].astype(jnp.float32)
            return unused, jnp.einsum("eps,sek->epk", picked, chosen)

        _, gradient = lax.scan(gradient_seg, jnp.float32(0.0), (columns, layout, slot_ids))
        shifted = current + step_scale * gradient
        shrunk = jnp.sign(shifted) * jnp.maximum(jnp.abs(shifted) - cutoff, jnp.float32(0.0))
        current = jnp.where(active[:, :, None, None], shrunk, jnp.float32(0.0))
    return current.reshape(N_SNP * NE, PT, SB)
```

```python
import jax
import jax.numpy as jnp
from jax import lax
from jax.sharding import PartitionSpec as P

ITERS = 2


step_scale = 0.3


def shrink_soft(current, gradient, cutoff, active):
    shifted = current + step_scale * gradient
    shrunk = jnp.sign(shifted) * jnp.maximum(jnp.abs(shifted) - cutoff, jnp.float32(0.0))
    return jnp.where(active[:, None, None], shrunk, jnp.float32(0.0))


def per_device(genotypes, responses, weights, pattern, entry_count, tile_slot, penalty):
    sample_count = genotypes.shape[0]
    entries, tile_width, block_width = weights.shape
    block_count = genotypes.shape[1] // block_width
    own_rows = responses.shape[0]
    owners = lax.axis_size("snp")
    own_slots = own_rows // tile_width
    slot_total = owners * own_slots
    cells = slot_total * block_count

    geno_blocks = genotypes.reshape(sample_count, block_count, block_width)
    blk = pattern[:, 0]
    tile = pattern[:, 1]
    tile_hot = tile[:, None] == jnp.arange(penalty.shape[0], dtype=jnp.int32)[None, :]
    slot_ids = jnp.sum(jnp.where(tile_hot, tile_slot[None, :], 0), axis=1)
    per_entry = jnp.sum(jnp.where(tile_hot, penalty[None, :], jnp.float32(0.0)), axis=1)
    cutoff = step_scale * per_entry[:, None, None]
    cell = slot_ids * block_count + blk
    cell_hot = (cell[:, None] == jnp.arange(cells, dtype=jnp.int32)[None, :]).astype(jnp.bfloat16)
    active = jnp.arange(entries, dtype=jnp.int32) < entry_count[0]
    current = jnp.where(active[:, None, None], weights, jnp.float32(0.0))
    for sweep in range(ITERS):
        weight_bf = current.astype(jnp.bfloat16)
        dense = jnp.einsum(
            "ec,epk->cpk", cell_hot, weight_bf, preferred_element_type=jnp.float32
        ).astype(jnp.bfloat16)
        dense = dense.reshape(slot_total, block_count, tile_width, block_width)
        partial = jnp.einsum(
            "jbpk,sbk->jps", dense, geno_blocks, preferred_element_type=jnp.float32
        ).astype(jnp.bfloat16)
        partial = partial.reshape(owners, own_rows, sample_count)
        gathered = lax.all_to_all(partial, "snp", 0, 0, tiled=False)
        prediction = jnp.sum(gathered.astype(jnp.float32), axis=0)
        residual = (responses - prediction).astype(jnp.bfloat16)
        shard_rows = lax.all_gather(residual, "snp", axis=0, tiled=True)
        blocks = shard_rows.reshape(slot_total, tile_width, sample_count)
        full = jnp.einsum(
            "jps,sbk->jbpk", blocks, geno_blocks, preferred_element_type=jnp.float32
        ).reshape(cells, tile_width, block_width)
        local_gradient = jnp.take(full, cell, axis=0, mode="clip")
        gradient = lax.psum(local_gradient, "samp")
        current = shrink_soft(current, gradient, cutoff, active)
    return current


def solution(mesh):
    in_specs = (
        P("samp", "snp"),
        P("snp", "samp"),
        P("snp", None, None),
        P("snp", None),
        P("snp"),
        P(),
        P(),
    )
    out_specs = P("snp", None, None)
    return jax.shard_map(
        per_device, mesh=mesh, in_specs=in_specs, out_specs=out_specs, check_vma=False
    )
```

```python
import jax
import jax.numpy as jnp
from jax import lax
from jax.sharding import PartitionSpec as P

ITERS = 2


step_scale = 0.3


def shrink_soft(current, gradient, cutoff, active):
    shifted = current + step_scale * gradient
    shrunk = jnp.sign(shifted) * jnp.maximum(jnp.abs(shifted) - cutoff, jnp.float32(0.0))
    return jnp.where(active[:, None, None], shrunk, jnp.float32(0.0))


def per_device(genotypes, responses, weights, pattern, entry_count, tile_slot, penalty):
    sample_count = genotypes.shape[0]
    entries, tile_width, block_width = weights.shape
    block_count = genotypes.shape[1] // block_width
    own_rows = responses.shape[0]
    owners = lax.axis_size("snp")
    own_slots = own_rows // tile_width
    slot_total = owners * own_slots
    cells = slot_total * block_count

    geno_blocks = genotypes.reshape(sample_count, block_count, block_width)
    blk = pattern[:, 0]
    tile = pattern[:, 1]
    tile_hot = tile[:, None] == jnp.arange(penalty.shape[0], dtype=jnp.int32)[None, :]
    slot_ids = jnp.sum(jnp.where(tile_hot, tile_slot[None, :], 0), axis=1)
    per_entry = jnp.sum(jnp.where(tile_hot, penalty[None, :], jnp.float32(0.0)), axis=1)
    cutoff = step_scale * per_entry[:, None, None]
    cell = slot_ids * block_count + blk
    cell_hot = (cell[:, None] == jnp.arange(cells, dtype=jnp.int32)[None, :]).astype(jnp.bfloat16)
    active = jnp.arange(entries, dtype=jnp.int32) < entry_count[0]
    current = jnp.where(active[:, None, None], weights, jnp.float32(0.0))
    for sweep in range(ITERS):
        weight_bf = current.astype(jnp.bfloat16)
        dense = jnp.einsum(
            "ec,epk->cpk", cell_hot, weight_bf, preferred_element_type=jnp.float32
        ).astype(jnp.bfloat16)
        dense = dense.reshape(slot_total, block_count, tile_width, block_width)
        partial = jnp.einsum(
            "jbpk,sbk->jps", dense, geno_blocks, preferred_element_type=jnp.float32
        ).astype(jnp.bfloat16)
        partial = partial.reshape(owners, own_rows, sample_count)
        gathered = lax.all_to_all(partial, "snp", 0, 0, tiled=False)
        prediction = jnp.sum(gathered.astype(jnp.float32), axis=0)
        residual = (responses - prediction).astype(jnp.bfloat16)
        shard_rows = lax.all_gather(residual, "snp", axis=0, tiled=True)
        blocks = shard_rows.reshape(slot_total, tile_width, sample_count)
        full = jnp.einsum(
            "jps,sbk->jbpk", blocks, geno_blocks, preferred_element_type=jnp.float32
        ).reshape(cells, tile_width, block_width)
        local_gradient = jnp.take(full, cell, axis=0, mode="clip")
        if SPLIT_SAMP:
            part = lax.psum_scatter(local_gradient, "sc", scatter_dimension=0, tiled=True)
            part = lax.psum(part, "sx")
            gradient = lax.all_gather(part, "sc", axis=0, tiled=True)
        else:
            gradient = lax.psum(local_gradient, "samp")
        current = shrink_soft(current, gradient, cutoff, active)
    return current


SPLIT_SAMP = True


def solution(mesh):
    snp_size, samp_size = mesh.devices.shape
    samp = "samp"
    if SPLIT_SAMP:
        devices = mesh.devices.reshape(snp_size, 2, samp_size // 2)
        mesh = jax.sharding.Mesh(devices, ("snp", "sx", "sc"))
        samp = ("sx", "sc")
    in_specs = (
        P(samp, "snp"),
        P("snp", samp),
        P("snp", None, None),
        P("snp", None),
        P("snp"),
        P(),
        P(),
    )
    out_specs = P("snp", None, None)
    return jax.shard_map(
        per_device, mesh=mesh, in_specs=in_specs, out_specs=out_specs, check_vma=False
    )
```

```python
import jax
import jax.numpy as jnp
from jax import lax
from jax.sharding import PartitionSpec as P

ITERS = 2


step_scale = 0.3


def shrink_soft(current, gradient, cutoff, active):
    shifted = current + step_scale * gradient
    shrunk = jnp.sign(shifted) * jnp.maximum(jnp.abs(shifted) - cutoff, jnp.float32(0.0))
    return jnp.where(active[:, None, None], shrunk, jnp.float32(0.0))


def per_device(genotypes, responses, weights, pattern, entry_count, tile_slot, penalty):
    sample_count = genotypes.shape[0]
    entries, tile_width, block_width = weights.shape
    block_count = genotypes.shape[1] // block_width
    own_rows = responses.shape[0]
    owners = lax.axis_size("snp")
    own_slots = own_rows // tile_width
    slot_total = owners * own_slots
    cells = slot_total * block_count

    geno_blocks = genotypes.reshape(sample_count, block_count, block_width)
    blk = pattern[:, 0]
    tile = pattern[:, 1]
    tile_hot = tile[:, None] == jnp.arange(penalty.shape[0], dtype=jnp.int32)[None, :]
    slot_ids = jnp.sum(jnp.where(tile_hot, tile_slot[None, :], 0), axis=1)
    per_entry = jnp.sum(jnp.where(tile_hot, penalty[None, :], jnp.float32(0.0)), axis=1)
    cutoff = step_scale * per_entry[:, None, None]
    cell = slot_ids * block_count + blk
    cell_hot = (cell[:, None] == jnp.arange(cells, dtype=jnp.int32)[None, :]).astype(jnp.bfloat16)
    active = jnp.arange(entries, dtype=jnp.int32) < entry_count[0]
    current = jnp.where(active[:, None, None], weights, jnp.float32(0.0))
    for sweep in range(ITERS):
        weight_bf = current.astype(jnp.bfloat16)
        dense = jnp.einsum(
            "ec,epk->cpk", cell_hot, weight_bf, preferred_element_type=jnp.float32
        ).astype(jnp.bfloat16)
        dense = dense.reshape(slot_total, block_count, tile_width, block_width)
        partial = jnp.einsum(
            "jbpk,sbk->jps", dense, geno_blocks, preferred_element_type=jnp.float32
        ).astype(jnp.bfloat16)
        partial = partial.reshape(owners, own_rows, sample_count)
        gathered = lax.all_to_all(partial, "snp", 0, 0, tiled=False)
        prediction = jnp.sum(gathered.astype(jnp.float32), axis=0)
        residual = (responses - prediction).astype(jnp.bfloat16)
        shard_rows = lax.all_gather(residual, "snp", axis=0, tiled=True)
        blocks = shard_rows.reshape(slot_total, tile_width, sample_count)
        full = jnp.einsum(
            "jps,sbk->jbpk", blocks, geno_blocks, preferred_element_type=jnp.float32
        ).reshape(cells, tile_width, block_width)
        local_gradient = jnp.take(full, cell, axis=0, mode="clip")
        gradient = lax.psum(local_gradient.astype(jnp.bfloat16), "samp").astype(jnp.float32)
        current = shrink_soft(current, gradient, cutoff, active)
    return current


def solution(mesh):
    in_specs = (
        P("samp", "snp"),
        P("snp", "samp"),
        P("snp", None, None),
        P("snp", None),
        P("snp"),
        P(),
        P(),
    )
    out_specs = P("snp", None, None)
    return jax.shard_map(
        per_device, mesh=mesh, in_specs=in_specs, out_specs=out_specs, check_vma=False
    )
```

```python
import jax
import jax.numpy as jnp
from jax import lax
from jax.sharding import PartitionSpec as P

ITERS = 2


step_scale = 0.3


def shrink_soft(current, gradient, cutoff, active):
    shifted = current + step_scale * gradient
    shrunk = jnp.sign(shifted) * jnp.maximum(jnp.abs(shifted) - cutoff, jnp.float32(0.0))
    return jnp.where(active[:, None, None], shrunk, jnp.float32(0.0))


def per_device(genotypes, responses, weights, pattern, entry_count, tile_slot, penalty):
    sample_count = genotypes.shape[0]
    entries, tile_width, block_width = weights.shape
    block_count = genotypes.shape[1] // block_width
    own_rows = responses.shape[0]
    owners = lax.axis_size("snp")
    own_slots = own_rows // tile_width
    slot_total = owners * own_slots
    cells = slot_total * block_count

    geno_blocks = genotypes.reshape(sample_count, block_count, block_width)
    blk = pattern[:, 0]
    tile = pattern[:, 1]
    tile_hot = tile[:, None] == jnp.arange(penalty.shape[0], dtype=jnp.int32)[None, :]
    slot_ids = jnp.sum(jnp.where(tile_hot, tile_slot[None, :], 0), axis=1)
    per_entry = jnp.sum(jnp.where(tile_hot, penalty[None, :], jnp.float32(0.0)), axis=1)
    cutoff = step_scale * per_entry[:, None, None]
    cell = slot_ids * block_count + blk
    cell_hot = (cell[:, None] == jnp.arange(cells, dtype=jnp.int32)[None, :]).astype(jnp.bfloat16)
    active = jnp.arange(entries, dtype=jnp.int32) < entry_count[0]
    current = jnp.where(active[:, None, None], weights, jnp.float32(0.0))
    weight_bf = current.astype(jnp.bfloat16)
    share = entries // lax.axis_size("samp")
    start = lax.axis_index("samp") * share
    own = lax.dynamic_slice_in_dim(current, start, share, 0)
    own_cutoff = lax.dynamic_slice_in_dim(cutoff, start, share, 0)
    own_active = lax.dynamic_slice_in_dim(active, start, share, 0)
    for sweep in range(ITERS):
        dense = jnp.einsum(
            "ec,epk->cpk", cell_hot, weight_bf, preferred_element_type=jnp.float32
        ).astype(jnp.bfloat16)
        dense = dense.reshape(slot_total, block_count, tile_width, block_width)
        partial = jnp.einsum(
            "jbpk,sbk->jps", dense, geno_blocks, preferred_element_type=jnp.float32
        ).astype(jnp.bfloat16)
        partial = partial.reshape(owners, own_rows, sample_count)
        gathered = lax.all_to_all(partial, "snp", 0, 0, tiled=False)
        prediction = jnp.sum(gathered.astype(jnp.float32), axis=0)
        residual = (responses - prediction).astype(jnp.bfloat16)
        shard_rows = lax.all_gather(residual, "snp", axis=0, tiled=True)
        blocks = shard_rows.reshape(slot_total, tile_width, sample_count)
        full = jnp.einsum(
            "jps,sbk->jbpk", blocks, geno_blocks, preferred_element_type=jnp.float32
        ).reshape(cells, tile_width, block_width)
        local_gradient = jnp.take(full, cell, axis=0, mode="clip")
        own_gradient = lax.psum_scatter(local_gradient, "samp", scatter_dimension=0, tiled=True)
        own = shrink_soft(own, own_gradient, own_cutoff, own_active)
        if sweep + 1 < ITERS:
            weight_bf = lax.all_gather(own.astype(jnp.bfloat16), "samp", axis=0, tiled=True)
    return lax.all_gather(own, "samp", axis=0, tiled=True)


def solution(mesh):
    in_specs = (
        P("samp", "snp"),
        P("snp", "samp"),
        P("snp", None, None),
        P("snp", None),
        P("snp"),
        P(),
        P(),
    )
    out_specs = P("snp", None, None)
    return jax.shard_map(
        per_device, mesh=mesh, in_specs=in_specs, out_specs=out_specs, check_vma=False
    )
```

```python
import jax
import jax.numpy as jnp
from jax import lax
from jax.sharding import PartitionSpec as P

ITERS = 2


step_scale = 0.3


def shrink_soft(current, gradient, cutoff, active):
    shifted = current + step_scale * gradient
    shrunk = jnp.sign(shifted) * jnp.maximum(jnp.abs(shifted) - cutoff, jnp.float32(0.0))
    return jnp.where(active[:, None, None], shrunk, jnp.float32(0.0))


def per_device(genotypes, responses, weights, pattern, entry_count, tile_slot, penalty):
    sample_count = genotypes.shape[0]
    entries, tile_width, block_width = weights.shape
    block_count = genotypes.shape[1] // block_width
    own_rows = responses.shape[0]
    owners = lax.axis_size("snp")
    own_slots = own_rows // tile_width
    slot_total = owners * own_slots
    cells = slot_total * block_count

    geno_blocks = genotypes.reshape(sample_count, block_count, block_width)
    blk = pattern[:, 0]
    tile = pattern[:, 1]
    tile_hot = tile[:, None] == jnp.arange(penalty.shape[0], dtype=jnp.int32)[None, :]
    slot_ids = jnp.sum(jnp.where(tile_hot, tile_slot[None, :], 0), axis=1)
    per_entry = jnp.sum(jnp.where(tile_hot, penalty[None, :], jnp.float32(0.0)), axis=1)
    cutoff = step_scale * per_entry[:, None, None]
    cell = slot_ids * block_count + blk
    cell_hot = (cell[:, None] == jnp.arange(cells, dtype=jnp.int32)[None, :]).astype(jnp.bfloat16)
    active = jnp.arange(entries, dtype=jnp.int32) < entry_count[0]
    current = jnp.where(active[:, None, None], weights, jnp.float32(0.0))
    weight_bf = current.astype(jnp.bfloat16)
    share = entries // lax.axis_size("samp")
    start = lax.axis_index("samp") * share
    own = lax.dynamic_slice_in_dim(current, start, share, 0)
    own_cutoff = lax.dynamic_slice_in_dim(cutoff, start, share, 0)
    own_active = lax.dynamic_slice_in_dim(active, start, share, 0)
    for sweep in range(ITERS):
        dense = jnp.einsum(
            "ec,epk->cpk", cell_hot, weight_bf, preferred_element_type=jnp.float32
        ).astype(jnp.bfloat16)
        dense = dense.reshape(slot_total, block_count, tile_width, block_width)
        partial = jnp.einsum(
            "jbpk,sbk->jps", dense, geno_blocks, preferred_element_type=jnp.float32
        ).astype(jnp.bfloat16)
        partial = partial.reshape(owners, own_rows, sample_count)
        gathered = lax.all_to_all(partial, "snp", 0, 0, tiled=False)
        prediction = jnp.sum(gathered.astype(jnp.float32), axis=0)
        residual = (responses - prediction).astype(jnp.bfloat16)
        shard_rows = lax.all_gather(residual, "snp", axis=0, tiled=True)
        blocks = shard_rows.reshape(slot_total, tile_width, sample_count)
        full = jnp.einsum(
            "jps,sbk->jbpk", blocks, geno_blocks, preferred_element_type=jnp.float32
        ).reshape(cells, tile_width, block_width)
        local_gradient = jnp.take(full, cell, axis=0, mode="clip")
        rows = local_gradient.reshape(entries * tile_width, block_width)
        mine = lax.psum_scatter(rows, "samp", scatter_dimension=0, tiled=True)
        own_gradient = mine.reshape(share, tile_width, block_width)
        own = shrink_soft(own, own_gradient, own_cutoff, own_active)
        if sweep + 1 < ITERS:
            flat = own.astype(jnp.bfloat16).reshape(share * tile_width, block_width)
            weight_bf = lax.all_gather(flat, "samp", axis=0, tiled=True).reshape(weights.shape)
    flat = own.reshape(share * tile_width, block_width)
    return lax.all_gather(flat, "samp", axis=0, tiled=True).reshape(weights.shape)


def solution(mesh):
    in_specs = (
        P("samp", "snp"),
        P("snp", "samp"),
        P("snp", None, None),
        P("snp", None),
        P("snp"),
        P(),
        P(),
    )
    out_specs = P("snp", None, None)
    return jax.shard_map(
        per_device, mesh=mesh, in_specs=in_specs, out_specs=out_specs, check_vma=False
    )
```

```python
import jax
import jax.numpy as jnp
from jax import lax
from jax.sharding import PartitionSpec as P

ITERS = 2


step_scale = 0.3


def shrink_soft(current, gradient, cutoff, active):
    shifted = current + step_scale * gradient
    shrunk = jnp.sign(shifted) * jnp.maximum(jnp.abs(shifted) - cutoff, jnp.float32(0.0))
    return jnp.where(active[:, None, None], shrunk, jnp.float32(0.0))


def per_device(genotypes, responses, weights, pattern, entry_count, tile_slot, penalty):
    quarter = genotypes.shape[0]
    entries, tile_width, block_width = weights.shape
    block_count = genotypes.shape[1] // block_width
    own_rows = responses.shape[0]
    owners = lax.axis_size("snp")
    own_slots = own_rows // tile_width
    slot_total = owners * own_slots
    cells = slot_total * block_count
    halves = lax.axis_size("sx")
    cores = lax.axis_size("sc")
    half_p = tile_width // halves
    x = lax.axis_index("sx")
    c = lax.axis_index("sc")

    geno = lax.all_gather(genotypes, "sx", axis=0, tiled=True)
    sample_count = geno.shape[0]
    geno_blocks = geno.reshape(sample_count, block_count, block_width)
    resp = responses.reshape(own_slots, halves, half_p, quarter)
    resp = jnp.moveaxis(resp, 1, 0)
    resp = lax.all_to_all(resp, "sx", 0, 0, tiled=False)
    resp = jnp.moveaxis(resp, 0, 2).reshape(own_slots * half_p, halves * quarter)

    blk = pattern[:, 0]
    tile = pattern[:, 1]
    tile_hot = tile[:, None] == jnp.arange(penalty.shape[0], dtype=jnp.int32)[None, :]
    slot_ids = jnp.sum(jnp.where(tile_hot, tile_slot[None, :], 0), axis=1)
    per_entry = jnp.sum(jnp.where(tile_hot, penalty[None, :], jnp.float32(0.0)), axis=1)
    cutoff = step_scale * per_entry[:, None, None]
    cell = slot_ids * block_count + blk
    cell_hot = (cell[:, None] == jnp.arange(cells, dtype=jnp.int32)[None, :]).astype(jnp.bfloat16)
    active = jnp.arange(entries, dtype=jnp.int32) < entry_count[0]
    w_half = lax.dynamic_slice_in_dim(weights, x * half_p, half_p, 1)
    weight_bf = jnp.where(active[:, None, None], w_half, jnp.float32(0.0)).astype(jnp.bfloat16)
    share = entries // cores
    start = c * share
    own_active = lax.dynamic_slice_in_dim(active, start, share, 0)
    own_cutoff = lax.dynamic_slice_in_dim(cutoff, start, share, 0)
    own = jnp.where(
        own_active[:, None, None],
        lax.dynamic_slice_in_dim(w_half, start, share, 0),
        jnp.float32(0.0),
    )
    for sweep in range(ITERS):
        dense = jnp.einsum(
            "ec,epk->cpk", cell_hot, weight_bf, preferred_element_type=jnp.float32
        ).astype(jnp.bfloat16)
        dense = dense.reshape(slot_total, block_count, half_p, block_width)
        partial = jnp.einsum(
            "jbpk,sbk->jps", dense, geno_blocks, preferred_element_type=jnp.float32
        ).astype(jnp.bfloat16)
        partial = partial.reshape(owners, own_slots * half_p, sample_count)
        gathered = lax.all_to_all(partial, "snp", 0, 0, tiled=False)
        prediction = jnp.sum(gathered.astype(jnp.float32), axis=0)
        residual = (resp - prediction).astype(jnp.bfloat16)
        shard_rows = lax.all_gather(residual, "snp", axis=0, tiled=True)
        blocks = shard_rows.reshape(slot_total, half_p, sample_count)
        full = jnp.einsum(
            "jps,sbk->jbpk", blocks, geno_blocks, preferred_element_type=jnp.float32
        ).reshape(cells, half_p, block_width)
        local_gradient = jnp.take(full, cell, axis=0, mode="clip")
        rows = local_gradient.reshape(entries * half_p, block_width)
        mine = lax.psum_scatter(rows, "sc", scatter_dimension=0, tiled=True)
        own_gradient = mine.reshape(share, half_p, block_width)
        own = shrink_soft(own, own_gradient, own_cutoff, own_active)
        if sweep + 1 < ITERS:
            flat = own.astype(jnp.bfloat16).reshape(share * half_p, block_width)
            weight_bf = lax.all_gather(flat, "sc", axis=0, tiled=True).reshape(
                entries, half_p, block_width
            )
    both = lax.all_gather(own, "sx", axis=1, tiled=True)
    flat = both.reshape(share * tile_width, block_width)
    return lax.all_gather(flat, "sc", axis=0, tiled=True).reshape(weights.shape)


def solution(mesh):
    snp_size, samp_size = mesh.devices.shape
    devices = mesh.devices.reshape(snp_size, 2, samp_size // 2)
    mesh = jax.sharding.Mesh(devices, ("snp", "sx", "sc"))
    samp = ("sx", "sc")
    in_specs = (
        P(samp, "snp"),
        P("snp", samp),
        P("snp", None, None),
        P("snp", None),
        P("snp"),
        P(),
        P(),
    )
    out_specs = P("snp", None, None)
    return jax.shard_map(
        per_device, mesh=mesh, in_specs=in_specs, out_specs=out_specs, check_vma=False
    )
```

```python
import jax
import jax.numpy as jnp
from jax import lax
from jax.sharding import PartitionSpec as P

ITERS = 2


step_scale = 0.3


def shrink_soft(current, gradient, cutoff, active):
    shifted = current + step_scale * gradient
    shrunk = jnp.sign(shifted) * jnp.maximum(jnp.abs(shifted) - cutoff, jnp.float32(0.0))
    return jnp.where(active[:, None, None], shrunk, jnp.float32(0.0))


def per_device(genotypes, responses, weights, pattern, entry_count, tile_slot, penalty):
    quarter = genotypes.shape[0]
    entries, tile_width, block_width = weights.shape
    block_count = genotypes.shape[1] // block_width
    own_rows = responses.shape[0]
    owners = lax.axis_size("snp")
    own_slots = own_rows // tile_width
    slot_total = owners * own_slots
    cells = slot_total * block_count
    halves = lax.axis_size("sx")
    cores = lax.axis_size("sc")
    half_p = tile_width // halves
    x = lax.axis_index("sx")
    c = lax.axis_index("sc")

    swap = [(0, 1), (1, 0)]
    geno_peer = lax.ppermute(genotypes, "sx", swap)
    geno = jnp.concatenate([genotypes, geno_peer], axis=0)
    sample_count = geno.shape[0]
    geno_blocks = geno.reshape(sample_count, block_count, block_width)
    resp4 = responses.reshape(own_slots, halves, half_p, quarter)
    resp_own = lax.dynamic_slice_in_dim(resp4, x, 1, 1)[:, 0]
    resp_peer = lax.ppermute(lax.dynamic_slice_in_dim(resp4, 1 - x, 1, 1)[:, 0], "sx", swap)
    resp = jnp.concatenate([resp_own, resp_peer], axis=2).reshape(
        own_slots * half_p, halves * quarter
    )

    blk = pattern[:, 0]
    tile = pattern[:, 1]
    tile_hot = tile[:, None] == jnp.arange(penalty.shape[0], dtype=jnp.int32)[None, :]
    slot_ids = jnp.sum(jnp.where(tile_hot, tile_slot[None, :], 0), axis=1)
    per_entry = jnp.sum(jnp.where(tile_hot, penalty[None, :], jnp.float32(0.0)), axis=1)
    cutoff = step_scale * per_entry[:, None, None]
    cell = slot_ids * block_count + blk
    cell_hot = (cell[:, None] == jnp.arange(cells, dtype=jnp.int32)[None, :]).astype(jnp.bfloat16)
    active = jnp.arange(entries, dtype=jnp.int32) < entry_count[0]
    w_half = lax.dynamic_slice_in_dim(weights, x * half_p, half_p, 1)
    weight_bf = jnp.where(active[:, None, None], w_half, jnp.float32(0.0)).astype(jnp.bfloat16)
    share = entries // cores
    start = c * share
    own_active = lax.dynamic_slice_in_dim(active, start, share, 0)
    own_cutoff = lax.dynamic_slice_in_dim(cutoff, start, share, 0)
    own = jnp.where(
        own_active[:, None, None],
        lax.dynamic_slice_in_dim(w_half, start, share, 0),
        jnp.float32(0.0),
    )
    for sweep in range(ITERS):
        dense = jnp.einsum(
            "ec,epk->cpk", cell_hot, weight_bf, preferred_element_type=jnp.float32
        ).astype(jnp.bfloat16)
        dense = dense.reshape(slot_total, block_count, half_p, block_width)

        def predict(samples):
            count = samples.shape[0]
            partial = jnp.einsum(
                "jbpk,sbk->jps",
                dense,
                samples.reshape(count, block_count, block_width),
                preferred_element_type=jnp.float32,
            ).astype(jnp.bfloat16)
            partial = partial.reshape(owners, own_slots * half_p, count)
            gathered = lax.all_to_all(partial, "snp", 0, 0, tiled=False)
            return jnp.sum(gathered.astype(jnp.float32), axis=0)

        if sweep == 0:
            prediction = jnp.concatenate([predict(genotypes), predict(geno_peer)], axis=1)
        else:
            prediction = predict(geno)
        residual = (resp - prediction).astype(jnp.bfloat16)
        shard_rows = lax.all_gather(residual, "snp", axis=0, tiled=True)
        blocks = shard_rows.reshape(slot_total, half_p, sample_count)
        full = jnp.einsum(
            "jps,sbk->jbpk", blocks, geno_blocks, preferred_element_type=jnp.float32
        ).reshape(cells, half_p, block_width)
        local_gradient = jnp.take(full, cell, axis=0, mode="clip")
        rows = local_gradient.reshape(entries * half_p, block_width)
        mine = lax.psum_scatter(rows, "sc", scatter_dimension=0, tiled=True)
        own_gradient = mine.reshape(share, half_p, block_width)
        own = shrink_soft(own, own_gradient, own_cutoff, own_active)
        if sweep + 1 < ITERS:
            flat = own.astype(jnp.bfloat16).reshape(share * half_p, block_width)
            weight_bf = lax.all_gather(flat, "sc", axis=0, tiled=True).reshape(
                entries, half_p, block_width
            )
    both = lax.all_gather(own, "sx", axis=1, tiled=True)
    flat = both.reshape(share * tile_width, block_width)
    return lax.all_gather(flat, "sc", axis=0, tiled=True).reshape(weights.shape)


def solution(mesh):
    snp_size, samp_size = mesh.devices.shape
    devices = mesh.devices.reshape(snp_size, 2, samp_size // 2)
    mesh = jax.sharding.Mesh(devices, ("snp", "sx", "sc"))
    samp = ("sx", "sc")
    in_specs = (
        P(samp, "snp"),
        P("snp", samp),
        P("snp", None, None),
        P("snp", None),
        P("snp"),
        P(),
        P(),
    )
    out_specs = P("snp", None, None)
    return jax.shard_map(
        per_device, mesh=mesh, in_specs=in_specs, out_specs=out_specs, check_vma=False
    )
```

```python
import jax
import jax.numpy as jnp
from jax import lax
from jax.sharding import PartitionSpec as P

ITERS = 2


step_scale = 0.3


def shrink_soft(current, gradient, cutoff, active):
    shifted = current + step_scale * gradient
    shrunk = jnp.sign(shifted) * jnp.maximum(jnp.abs(shifted) - cutoff, jnp.float32(0.0))
    return jnp.where(active[:, None, None], shrunk, jnp.float32(0.0))


def per_device(genotypes, responses, weights, pattern, entry_count, tile_slot, penalty):
    quarter = genotypes.shape[0]
    entries, tile_width, block_width = weights.shape
    block_count = genotypes.shape[1] // block_width
    own_rows = responses.shape[0]
    owners = lax.axis_size("snp")
    own_slots = own_rows // tile_width
    slot_total = owners * own_slots
    cells = slot_total * block_count
    halves = lax.axis_size("sx")
    cores = lax.axis_size("sc")
    half_p = tile_width // halves
    x = lax.axis_index("sx")
    c = lax.axis_index("sc")

    swap = [(0, 1), (1, 0)]
    geno_peer = lax.ppermute(genotypes, "sx", swap)
    geno = jnp.concatenate([genotypes, geno_peer], axis=0)
    sample_count = geno.shape[0]
    geno_blocks = geno.reshape(sample_count, block_count, block_width)
    resp4 = responses.reshape(own_slots, halves, half_p, quarter)
    resp_own = lax.dynamic_slice_in_dim(resp4, x, 1, 1)[:, 0]
    resp_peer = lax.ppermute(lax.dynamic_slice_in_dim(resp4, 1 - x, 1, 1)[:, 0], "sx", swap)
    resp = jnp.concatenate([resp_own, resp_peer], axis=2).reshape(
        own_slots * half_p, halves * quarter
    )

    blk = pattern[:, 0]
    tile = pattern[:, 1]
    tile_hot = tile[:, None] == jnp.arange(penalty.shape[0], dtype=jnp.int32)[None, :]
    slot_ids = jnp.sum(jnp.where(tile_hot, tile_slot[None, :], 0), axis=1)
    per_entry = jnp.sum(jnp.where(tile_hot, penalty[None, :], jnp.float32(0.0)), axis=1)
    cutoff = step_scale * per_entry[:, None, None]
    cell = slot_ids * block_count + blk
    cell_hot = (cell[:, None] == jnp.arange(cells, dtype=jnp.int32)[None, :]).astype(jnp.bfloat16)
    active = jnp.arange(entries, dtype=jnp.int32) < entry_count[0]
    w_half = lax.dynamic_slice_in_dim(weights, x * half_p, half_p, 1)
    weight_bf = jnp.where(active[:, None, None], w_half, jnp.float32(0.0)).astype(jnp.bfloat16)
    share = entries // cores
    start = c * share
    own_active = lax.dynamic_slice_in_dim(active, start, share, 0)
    own_cutoff = lax.dynamic_slice_in_dim(cutoff, start, share, 0)
    own = jnp.where(
        own_active[:, None, None],
        lax.dynamic_slice_in_dim(w_half, start, share, 0),
        jnp.float32(0.0),
    )
    for sweep in range(ITERS):
        dense = jnp.einsum(
            "ec,epk->cpk", cell_hot, weight_bf, preferred_element_type=jnp.float32
        ).astype(jnp.bfloat16)
        dense = dense.reshape(slot_total, block_count, half_p, block_width)

        def predict(samples):
            count = samples.shape[0]
            partial = jnp.einsum(
                "jbpk,sbk->jps",
                dense,
                samples.reshape(count, block_count, block_width),
                preferred_element_type=jnp.float32,
            ).astype(jnp.bfloat16)
            partial = partial.reshape(owners, own_slots * half_p, count)
            gathered = lax.all_to_all(partial, "snp", 0, 0, tiled=False)
            return jnp.sum(gathered.astype(jnp.float32), axis=0)

        if sweep == 0:
            prediction = jnp.concatenate([predict(genotypes), predict(geno_peer)], axis=1)
        else:
            prediction = predict(geno)
        residual = (resp - prediction).astype(jnp.bfloat16)
        shard_rows = lax.all_gather(residual, "snp", axis=0, tiled=True)
        blocks = shard_rows.reshape(slot_total, half_p, sample_count)
        full = jnp.einsum(
            "jps,sbk->jbpk", blocks, geno_blocks, preferred_element_type=jnp.float32
        ).reshape(cells, half_p, block_width)
        local_gradient = jnp.take(full, cell, axis=0, mode="clip")
        rows = local_gradient.reshape(entries * half_p, block_width)
        mine = lax.psum_scatter(rows, "sc", scatter_dimension=0, tiled=True)
        own_gradient = mine.reshape(share, half_p, block_width)
        own = shrink_soft(own, own_gradient, own_cutoff, own_active)
        if sweep + 1 < ITERS:
            flat = own.astype(jnp.bfloat16).reshape(share * half_p, block_width)
            weight_bf = lax.all_gather(flat, "sc", axis=0, tiled=True).reshape(
                entries, half_p, block_width
            )
    other_half = lax.ppermute(own, "sx", swap)
    mine = jnp.where(
        x == 0,
        jnp.concatenate([own, other_half], axis=1),
        jnp.concatenate([other_half, own], axis=1),
    )
    other_entries = lax.ppermute(mine, "sc", swap)
    return jnp.where(
        c == 0,
        jnp.concatenate([mine, other_entries], axis=0),
        jnp.concatenate([other_entries, mine], axis=0),
    )


def solution(mesh):
    snp_size, samp_size = mesh.devices.shape
    devices = mesh.devices.reshape(snp_size, 2, samp_size // 2)
    mesh = jax.sharding.Mesh(devices, ("snp", "sx", "sc"))
    samp = ("sx", "sc")
    in_specs = (
        P(samp, "snp"),
        P("snp", samp),
        P("snp", None, None),
        P("snp", None),
        P("snp"),
        P(),
        P(),
    )
    out_specs = P("snp", None, None)
    return jax.shard_map(
        per_device, mesh=mesh, in_specs=in_specs, out_specs=out_specs, check_vma=False
    )
```

```python
import jax
import jax.numpy as jnp
from jax import lax
from jax.sharding import PartitionSpec as P

ITERS = 2


step_scale = 0.3


def shrink_soft(current, gradient, cutoff, active):
    shifted = current + step_scale * gradient
    shrunk = jnp.sign(shifted) * jnp.maximum(jnp.abs(shifted) - cutoff, jnp.float32(0.0))
    return jnp.where(active[:, None, None], shrunk, jnp.float32(0.0))


def per_device(genotypes, responses, weights, pattern, entry_count, tile_slot, penalty):
    quarter = genotypes.shape[0]
    entries, tile_width, block_width = weights.shape
    block_count = genotypes.shape[1] // block_width
    own_rows = responses.shape[0]
    owners = lax.axis_size("snp")
    own_slots = own_rows // tile_width
    slot_total = owners * own_slots
    cells = slot_total * block_count
    halves = lax.axis_size("sx")
    cores = lax.axis_size("sc")
    half_p = tile_width // halves
    x = lax.axis_index("sx")
    c = lax.axis_index("sc")

    swap = [(0, 1), (1, 0)]
    geno_peer = lax.ppermute(genotypes, "sx", swap)
    geno = jnp.concatenate([genotypes, geno_peer], axis=0)
    sample_count = geno.shape[0]
    geno_blocks = geno.reshape(sample_count, block_count, block_width)
    resp4 = responses.reshape(own_slots, halves, half_p, quarter)
    resp_own = lax.dynamic_slice_in_dim(resp4, x, 1, 1)[:, 0]
    resp_peer = lax.ppermute(lax.dynamic_slice_in_dim(resp4, 1 - x, 1, 1)[:, 0], "sx", swap)
    resp = jnp.concatenate([resp_own, resp_peer], axis=2).reshape(
        own_slots * half_p, halves * quarter
    )

    blk = pattern[:, 0]
    tile = pattern[:, 1]
    tile_hot = tile[:, None] == jnp.arange(penalty.shape[0], dtype=jnp.int32)[None, :]
    slot_ids = jnp.sum(jnp.where(tile_hot, tile_slot[None, :], 0), axis=1)
    per_entry = jnp.sum(jnp.where(tile_hot, penalty[None, :], jnp.float32(0.0)), axis=1)
    cutoff = step_scale * per_entry[:, None, None]
    cell = slot_ids * block_count + blk
    cell_hot = (cell[:, None] == jnp.arange(cells, dtype=jnp.int32)[None, :]).astype(jnp.bfloat16)
    active = jnp.arange(entries, dtype=jnp.int32) < entry_count[0]
    w_half = lax.dynamic_slice_in_dim(weights, x * half_p, half_p, 1)
    weight_bf = jnp.where(active[:, None, None], w_half, jnp.float32(0.0)).astype(jnp.bfloat16)
    share = entries // cores
    start = c * share
    own_active = lax.dynamic_slice_in_dim(active, start, share, 0)
    own_cutoff = lax.dynamic_slice_in_dim(cutoff, start, share, 0)
    own = jnp.where(
        own_active[:, None, None],
        lax.dynamic_slice_in_dim(w_half, start, share, 0),
        jnp.float32(0.0),
    )
    for sweep in range(ITERS):
        dense = jnp.einsum(
            "ec,epk->cpk", cell_hot, weight_bf, preferred_element_type=jnp.float32
        ).astype(jnp.bfloat16)
        dense = dense.reshape(slot_total, block_count, half_p, block_width)

        def predict(samples):
            count = samples.shape[0]
            partial = jnp.einsum(
                "jbpk,sbk->jps",
                dense,
                samples.reshape(count, block_count, block_width),
                preferred_element_type=jnp.float32,
            ).astype(jnp.bfloat16)
            partial = partial.reshape(owners, own_slots * half_p, count)
            gathered = lax.all_to_all(partial, "snp", 0, 0, tiled=False)
            return jnp.sum(gathered.astype(jnp.float32), axis=0)

        if sweep == 0:
            prediction = jnp.concatenate([predict(genotypes), predict(geno_peer)], axis=1)
        else:
            prediction = predict(geno)
        residual = (resp - prediction).astype(jnp.bfloat16)
        shard_rows = lax.all_gather(residual, "snp", axis=0, tiled=True)
        blocks = shard_rows.reshape(slot_total, half_p, sample_count)
        full = jnp.einsum(
            "jps,sbk->jbpk", blocks, geno_blocks, preferred_element_type=jnp.float32
        ).reshape(cells, half_p, block_width)
        local_gradient = jnp.take(full, cell, axis=0, mode="clip")
        split = local_gradient.reshape(cores, share, half_p, block_width)
        keep = lax.dynamic_index_in_dim(split, c, 0, keepdims=False)
        give = lax.dynamic_index_in_dim(split, 1 - c, 0, keepdims=False)
        own_gradient = keep + lax.ppermute(give, "sc", swap)
        own = shrink_soft(own, own_gradient, own_cutoff, own_active)
        if sweep + 1 < ITERS:
            own_bf = own.astype(jnp.bfloat16)
            other_bf = lax.ppermute(own_bf, "sc", swap)
            weight_bf = jnp.where(
                c == 0,
                jnp.concatenate([own_bf, other_bf], axis=0),
                jnp.concatenate([other_bf, own_bf], axis=0),
            )
    other_half = lax.ppermute(own, "sx", swap)
    mine = jnp.where(
        x == 0,
        jnp.concatenate([own, other_half], axis=1),
        jnp.concatenate([other_half, own], axis=1),
    )
    other_entries = lax.ppermute(mine, "sc", swap)
    return jnp.where(
        c == 0,
        jnp.concatenate([mine, other_entries], axis=0),
        jnp.concatenate([other_entries, mine], axis=0),
    )


def solution(mesh):
    snp_size, samp_size = mesh.devices.shape
    devices = mesh.devices.reshape(snp_size, 2, samp_size // 2)
    mesh = jax.sharding.Mesh(devices, ("snp", "sx", "sc"))
    samp = ("sx", "sc")
    in_specs = (
        P(samp, "snp"),
        P("snp", samp),
        P("snp", None, None),
        P("snp", None),
        P("snp"),
        P(),
        P(),
    )
    out_specs = P("snp", None, None)
    return jax.shard_map(
        per_device, mesh=mesh, in_specs=in_specs, out_specs=out_specs, check_vma=False
    )
```

```python
import jax
import jax.numpy as jnp
from jax import lax
from jax.sharding import PartitionSpec as P

ITERS = 2


step_scale = 0.3


def shrink_soft(current, gradient, cutoff, active):
    shifted = current + step_scale * gradient
    shrunk = jnp.sign(shifted) * jnp.maximum(jnp.abs(shifted) - cutoff, jnp.float32(0.0))
    return jnp.where(active[:, None, None], shrunk, jnp.float32(0.0))


def per_device(genotypes, responses, weights, pattern, entry_count, tile_slot, penalty):
    quarter = genotypes.shape[0]
    entries, tile_width, block_width = weights.shape
    block_count = genotypes.shape[1] // block_width
    own_rows = responses.shape[0]
    owners = lax.axis_size("snp")
    own_slots = own_rows // tile_width
    slot_total = owners * own_slots
    cells = slot_total * block_count
    halves = lax.axis_size("sx")
    cores = lax.axis_size("sc")
    half_p = tile_width // halves
    x = lax.axis_index("sx")
    c = lax.axis_index("sc")

    swap = [(0, 1), (1, 0)]
    geno_peer = lax.ppermute(genotypes, "sx", swap)
    geno = jnp.concatenate([genotypes, geno_peer], axis=0)
    sample_count = geno.shape[0]
    geno_blocks = geno.reshape(sample_count, block_count, block_width)
    resp4 = responses.reshape(own_slots, halves, half_p, quarter)
    resp_own = lax.dynamic_slice_in_dim(resp4, x, 1, 1)[:, 0]
    resp_peer = lax.ppermute(lax.dynamic_slice_in_dim(resp4, 1 - x, 1, 1)[:, 0], "sx", swap)
    resp = jnp.concatenate([resp_own, resp_peer], axis=2).reshape(
        own_slots * half_p, halves * quarter
    )

    blk = pattern[:, 0]
    tile = pattern[:, 1]
    tile_hot = tile[:, None] == jnp.arange(penalty.shape[0], dtype=jnp.int32)[None, :]
    slot_ids = jnp.sum(jnp.where(tile_hot, tile_slot[None, :], 0), axis=1)
    per_entry = jnp.sum(jnp.where(tile_hot, penalty[None, :], jnp.float32(0.0)), axis=1)
    cutoff = step_scale * per_entry[:, None, None]
    cell = slot_ids * block_count + blk
    cell_hot = (cell[:, None] == jnp.arange(cells, dtype=jnp.int32)[None, :]).astype(jnp.bfloat16)
    ring = list(range(0, owners, 2)) + list(range(owners - 1, 0, -2))
    ring_pos = [0] * owners
    for k, dev in enumerate(ring):
        ring_pos[dev] = k
    forward = [(ring[k], ring[(k + 1) % owners]) for k in range(owners)]
    backward = [(ring[k], ring[(k - 1) % owners]) for k in range(owners)]
    forward_steps = owners // 2
    ring_table = jnp.asarray(ring_pos, dtype=jnp.int32)
    here = ring_table[lax.axis_index("snp")]
    rel_owner = (ring_table[slot_ids // own_slots] - here) % owners
    ring_cell = (rel_owner * own_slots + slot_ids % own_slots) * block_count + blk
    active = jnp.arange(entries, dtype=jnp.int32) < entry_count[0]
    w_half = lax.dynamic_slice_in_dim(weights, x * half_p, half_p, 1)
    weight_bf = jnp.where(active[:, None, None], w_half, jnp.float32(0.0)).astype(jnp.bfloat16)
    share = entries // cores
    start = c * share
    own_active = lax.dynamic_slice_in_dim(active, start, share, 0)
    own_cutoff = lax.dynamic_slice_in_dim(cutoff, start, share, 0)
    own = jnp.where(
        own_active[:, None, None],
        lax.dynamic_slice_in_dim(w_half, start, share, 0),
        jnp.float32(0.0),
    )
    for sweep in range(ITERS):
        dense = jnp.einsum(
            "ec,epk->cpk", cell_hot, weight_bf, preferred_element_type=jnp.float32
        ).astype(jnp.bfloat16)
        dense = dense.reshape(slot_total, block_count, half_p, block_width)

        def predict(samples):
            count = samples.shape[0]
            partial = jnp.einsum(
                "jbpk,sbk->jps",
                dense,
                samples.reshape(count, block_count, block_width),
                preferred_element_type=jnp.float32,
            ).astype(jnp.bfloat16)
            partial = partial.reshape(owners, own_slots * half_p, count)
            gathered = lax.all_to_all(partial, "snp", 0, 0, tiled=False)
            return jnp.sum(gathered.astype(jnp.float32), axis=0)

        if sweep == 0:
            prediction = jnp.concatenate([predict(genotypes), predict(geno_peer)], axis=1)
        else:
            prediction = predict(geno)
        residual = (resp - prediction).astype(jnp.bfloat16)
        received = {0: residual}
        moving = residual
        for step in range(1, forward_steps + 1):
            moving = lax.ppermute(moving, "snp", forward)
            received[owners - step] = moving
        moving = residual
        for step in range(1, owners - forward_steps):
            moving = lax.ppermute(moving, "snp", backward)
            received[step] = moving
        shard_rows = jnp.stack([received[d] for d in range(owners)])
        blocks = shard_rows.reshape(slot_total, half_p, sample_count)
        full = jnp.einsum(
            "jps,sbk->jbpk", blocks, geno_blocks, preferred_element_type=jnp.float32
        ).reshape(cells, half_p, block_width)
        local_gradient = jnp.take(full, ring_cell, axis=0, mode="clip")
        split = local_gradient.reshape(cores, share, half_p, block_width)
        keep = lax.dynamic_index_in_dim(split, c, 0, keepdims=False)
        give = lax.dynamic_index_in_dim(split, 1 - c, 0, keepdims=False)
        own_gradient = keep + lax.ppermute(give, "sc", swap)
        own = shrink_soft(own, own_gradient, own_cutoff, own_active)
        if sweep + 1 < ITERS:
            own_bf = own.astype(jnp.bfloat16)
            other_bf = lax.ppermute(own_bf, "sc", swap)
            weight_bf = jnp.where(
                c == 0,
                jnp.concatenate([own_bf, other_bf], axis=0),
                jnp.concatenate([other_bf, own_bf], axis=0),
            )
    other_half = lax.ppermute(own, "sx", swap)
    mine = jnp.where(
        x == 0,
        jnp.concatenate([own, other_half], axis=1),
        jnp.concatenate([other_half, own], axis=1),
    )
    other_entries = lax.ppermute(mine, "sc", swap)
    return jnp.where(
        c == 0,
        jnp.concatenate([mine, other_entries], axis=0),
        jnp.concatenate([other_entries, mine], axis=0),
    )


def solution(mesh):
    snp_size, samp_size = mesh.devices.shape
    devices = mesh.devices.reshape(snp_size, 2, samp_size // 2)
    mesh = jax.sharding.Mesh(devices, ("snp", "sx", "sc"))
    samp = ("sx", "sc")
    in_specs = (
        P(samp, "snp"),
        P("snp", samp),
        P("snp", None, None),
        P("snp", None),
        P("snp"),
        P(),
        P(),
    )
    out_specs = P("snp", None, None)
    return jax.shard_map(
        per_device, mesh=mesh, in_specs=in_specs, out_specs=out_specs, check_vma=False
    )
```

```python
import jax
import jax.numpy as jnp
from jax import lax
from jax.sharding import PartitionSpec as P

ITERS = 2


step_scale = 0.3


def shrink_soft(current, gradient, cutoff, active):
    shifted = current + step_scale * gradient
    shrunk = jnp.sign(shifted) * jnp.maximum(jnp.abs(shifted) - cutoff, jnp.float32(0.0))
    return jnp.where(active[:, None, None], shrunk, jnp.float32(0.0))


def per_device(genotypes, responses, weights, pattern, entry_count, tile_slot, penalty):
    quarter = genotypes.shape[0]
    entries, tile_width, block_width = weights.shape
    block_count = genotypes.shape[1] // block_width
    own_rows = responses.shape[0]
    owners = lax.axis_size("snp")
    own_slots = own_rows // tile_width
    slot_total = owners * own_slots
    cells = slot_total * block_count
    halves = lax.axis_size("sx")
    cores = lax.axis_size("sc")
    half_p = tile_width // halves
    x = lax.axis_index("sx")
    c = lax.axis_index("sc")

    swap = [(0, 1), (1, 0)]
    geno_peer = lax.ppermute(genotypes, "sx", swap)
    geno = jnp.concatenate([genotypes, geno_peer], axis=0)
    sample_count = geno.shape[0]
    geno_blocks = geno.reshape(sample_count, block_count, block_width)
    resp4 = responses.reshape(own_slots, halves, half_p, quarter)
    resp_own = lax.dynamic_slice_in_dim(resp4, x, 1, 1)[:, 0]
    resp_peer = lax.ppermute(lax.dynamic_slice_in_dim(resp4, 1 - x, 1, 1)[:, 0], "sx", swap)
    resp = jnp.concatenate([resp_own, resp_peer], axis=2).reshape(
        own_slots * half_p, halves * quarter
    )

    blk = pattern[:, 0]
    tile = pattern[:, 1]
    tile_hot = tile[:, None] == jnp.arange(penalty.shape[0], dtype=jnp.int32)[None, :]
    slot_ids = jnp.sum(jnp.where(tile_hot, tile_slot[None, :], 0), axis=1)
    per_entry = jnp.sum(jnp.where(tile_hot, penalty[None, :], jnp.float32(0.0)), axis=1)
    cutoff = step_scale * per_entry[:, None, None]
    cell = slot_ids * block_count + blk
    cell_hot = (cell[:, None] == jnp.arange(cells, dtype=jnp.int32)[None, :]).astype(jnp.bfloat16)
    ring = list(range(0, owners, 2)) + list(range(owners - 1, 0, -2))
    ring_pos = [0] * owners
    for k, dev in enumerate(ring):
        ring_pos[dev] = k
    forward = [(ring[k], ring[(k + 1) % owners]) for k in range(owners)]
    backward = [(ring[k], ring[(k - 1) % owners]) for k in range(owners)]
    forward_steps = owners // 2
    ring_table = jnp.asarray(ring_pos, dtype=jnp.int32)
    here = ring_table[lax.axis_index("snp")]
    rel_owner = (ring_table[slot_ids // own_slots] - here) % owners
    ring_slot = rel_owner * own_slots + slot_ids % own_slots
    active = jnp.arange(entries, dtype=jnp.int32) < entry_count[0]
    w_half = lax.dynamic_slice_in_dim(weights, x * half_p, half_p, 1)
    weight_bf = jnp.where(active[:, None, None], w_half, jnp.float32(0.0)).astype(jnp.bfloat16)
    share = entries // cores
    start = c * share
    own_active = lax.dynamic_slice_in_dim(active, start, share, 0)
    own_cutoff = lax.dynamic_slice_in_dim(cutoff, start, share, 0)
    own = jnp.where(
        own_active[:, None, None],
        lax.dynamic_slice_in_dim(w_half, start, share, 0),
        jnp.float32(0.0),
    )
    for sweep in range(ITERS):
        dense = jnp.einsum(
            "ec,epk->cpk", cell_hot, weight_bf, preferred_element_type=jnp.float32
        ).astype(jnp.bfloat16)
        dense = dense.reshape(slot_total, block_count, half_p, block_width)

        def predict(samples):
            count = samples.shape[0]
            partial = jnp.einsum(
                "jbpk,sbk->jps",
                dense,
                samples.reshape(count, block_count, block_width),
                preferred_element_type=jnp.float32,
            ).astype(jnp.bfloat16)
            partial = partial.reshape(owners, own_slots * half_p, count)
            gathered = lax.all_to_all(partial, "snp", 0, 0, tiled=False)
            return jnp.sum(gathered.astype(jnp.float32), axis=0)

        if sweep == 0:
            prediction = jnp.concatenate([predict(genotypes), predict(geno_peer)], axis=1)
        else:
            prediction = predict(geno)
        residual = (resp - prediction).astype(jnp.bfloat16)
        received = {0: residual}
        moving = residual
        for step in range(1, forward_steps + 1):
            moving = lax.ppermute(moving, "snp", forward)
            received[owners - step] = moving
        moving = residual
        for step in range(1, owners - forward_steps):
            moving = lax.ppermute(moving, "snp", backward)
            received[step] = moving
        shard_rows = jnp.stack([received[d] for d in range(owners)])
        blocks = shard_rows.reshape(slot_total, half_p, sample_count)
        full = jnp.einsum(
            "jps,sbk->jpbk", blocks, geno_blocks, preferred_element_type=jnp.float32
        )
        local_gradient = full[ring_slot, :, blk, :]
        split = local_gradient.reshape(cores, share, half_p, block_width)
        keep = lax.dynamic_index_in_dim(split, c, 0, keepdims=False)
        give = lax.dynamic_index_in_dim(split, 1 - c, 0, keepdims=False)
        own_gradient = keep + lax.ppermute(give, "sc", swap)
        own = shrink_soft(own, own_gradient, own_cutoff, own_active)
        if sweep + 1 < ITERS:
            own_bf = own.astype(jnp.bfloat16)
            other_bf = lax.ppermute(own_bf, "sc", swap)
            weight_bf = jnp.where(
                c == 0,
                jnp.concatenate([own_bf, other_bf], axis=0),
                jnp.concatenate([other_bf, own_bf], axis=0),
            )
    other_half = lax.ppermute(own, "sx", swap)
    mine = jnp.where(
        x == 0,
        jnp.concatenate([own, other_half], axis=1),
        jnp.concatenate([other_half, own], axis=1),
    )
    other_entries = lax.ppermute(mine, "sc", swap)
    return jnp.where(
        c == 0,
        jnp.concatenate([mine, other_entries], axis=0),
        jnp.concatenate([other_entries, mine], axis=0),
    )


def solution(mesh):
    snp_size, samp_size = mesh.devices.shape
    devices = mesh.devices.reshape(snp_size, 2, samp_size // 2)
    mesh = jax.sharding.Mesh(devices, ("snp", "sx", "sc"))
    samp = ("sx", "sc")
    in_specs = (
        P(samp, "snp"),
        P("snp", samp),
        P("snp", None, None),
        P("snp", None),
        P("snp"),
        P(),
        P(),
    )
    out_specs = P("snp", None, None)
    return jax.shard_map(
        per_device, mesh=mesh, in_specs=in_specs, out_specs=out_specs, check_vma=False
    )
```

```python
import jax
import jax.numpy as jnp
from jax import lax
from jax.sharding import PartitionSpec as P

ITERS = 2


step_scale = 0.3


def shrink_soft(current, gradient, cutoff, active):
    shifted = current + step_scale * gradient
    shrunk = jnp.sign(shifted) * jnp.maximum(jnp.abs(shifted) - cutoff, jnp.float32(0.0))
    return jnp.where(active[:, None, None], shrunk, jnp.float32(0.0))


def per_device(genotypes, responses, weights, pattern, entry_count, tile_slot, penalty):
    quarter = genotypes.shape[0]
    entries, tile_width, block_width = weights.shape
    block_count = genotypes.shape[1] // block_width
    own_rows = responses.shape[0]
    owners = lax.axis_size("snp")
    own_slots = own_rows // tile_width
    slot_total = owners * own_slots
    cells = slot_total * block_count
    halves = lax.axis_size("sx")
    cores = lax.axis_size("sc")
    half_p = tile_width // halves
    x = lax.axis_index("sx")
    c = lax.axis_index("sc")

    swap = [(0, 1), (1, 0)]
    geno_peer = lax.ppermute(genotypes, "sx", swap)
    geno = jnp.concatenate([genotypes, geno_peer], axis=0)
    sample_count = geno.shape[0]
    geno_blocks = geno.reshape(sample_count, block_count, block_width)
    resp4 = responses.reshape(own_slots, halves, half_p, quarter)
    resp_own = lax.dynamic_slice_in_dim(resp4, x, 1, 1)[:, 0]
    resp_peer = lax.ppermute(lax.dynamic_slice_in_dim(resp4, 1 - x, 1, 1)[:, 0], "sx", swap)
    resp = jnp.concatenate([resp_own, resp_peer], axis=2).reshape(
        own_slots * half_p, halves * quarter
    )

    blk = pattern[:, 0]
    tile = pattern[:, 1]
    tile_hot = tile[:, None] == jnp.arange(penalty.shape[0], dtype=jnp.int32)[None, :]
    slot_ids = jnp.sum(jnp.where(tile_hot, tile_slot[None, :], 0), axis=1)
    per_entry = jnp.sum(jnp.where(tile_hot, penalty[None, :], jnp.float32(0.0)), axis=1)
    cutoff = step_scale * per_entry[:, None, None]
    cell = slot_ids * block_count + blk
    cell_hot = (cell[:, None] == jnp.arange(cells, dtype=jnp.int32)[None, :]).astype(jnp.bfloat16)
    ring = list(range(0, owners, 2)) + list(range(owners - 1, 0, -2))
    ring_pos = [0] * owners
    for k, dev in enumerate(ring):
        ring_pos[dev] = k
    forward = [(ring[k], ring[(k + 1) % owners]) for k in range(owners)]
    backward = [(ring[k], ring[(k - 1) % owners]) for k in range(owners)]
    forward_steps = owners // 2
    ring_table = jnp.asarray(ring_pos, dtype=jnp.int32)
    ring_order = jnp.asarray(ring, dtype=jnp.int32)
    here = ring_table[lax.axis_index("snp")]
    rel_owner = (ring_table[slot_ids // own_slots] - here) % owners
    ring_slot = rel_owner * own_slots + slot_ids % own_slots
    active = jnp.arange(entries, dtype=jnp.int32) < entry_count[0]
    w_half = lax.dynamic_slice_in_dim(weights, x * half_p, half_p, 1)
    weight_bf = jnp.where(active[:, None, None], w_half, jnp.float32(0.0)).astype(jnp.bfloat16)
    share = entries // cores
    start = c * share
    own_active = lax.dynamic_slice_in_dim(active, start, share, 0)
    own_cutoff = lax.dynamic_slice_in_dim(cutoff, start, share, 0)
    own = jnp.where(
        own_active[:, None, None],
        lax.dynamic_slice_in_dim(w_half, start, share, 0),
        jnp.float32(0.0),
    )
    for sweep in range(ITERS):
        dense = jnp.einsum(
            "ec,epk->cpk", cell_hot, weight_bf, preferred_element_type=jnp.float32
        ).astype(jnp.bfloat16)
        dense = dense.reshape(slot_total, block_count, half_p, block_width)

        partial = jnp.einsum(
            "jbpk,sbk->jps", dense, geno_blocks, preferred_element_type=jnp.float32
        ).astype(jnp.bfloat16)
        partial = partial.reshape(owners, own_slots * half_p, sample_count)

        def owner_block(distance):
            owner = ring_order[(here + distance) % owners]
            return lax.dynamic_index_in_dim(partial, owner, 0, keepdims=False)

        ahead = lax.ppermute(owner_block(forward_steps), "snp", forward).astype(jnp.float32)
        for step in range(2, forward_steps + 1):
            carry = ahead + owner_block(forward_steps - step + 1).astype(jnp.float32)
            ahead = lax.ppermute(carry, "snp", forward)
        prediction = owner_block(0).astype(jnp.float32) + ahead
        behind_steps = owners - 1 - forward_steps
        if behind_steps > 0:
            behind = lax.ppermute(owner_block(-behind_steps), "snp", backward).astype(jnp.float32)
            for step in range(2, behind_steps + 1):
                carry = behind + owner_block(step - behind_steps - 1).astype(jnp.float32)
                behind = lax.ppermute(carry, "snp", backward)
            prediction = prediction + behind
        residual = (resp - prediction).astype(jnp.bfloat16)
        received = {0: residual}
        moving = residual
        for step in range(1, forward_steps + 1):
            moving = lax.ppermute(moving, "snp", forward)
            received[owners - step] = moving
        moving = residual
        for step in range(1, owners - forward_steps):
            moving = lax.ppermute(moving, "snp", backward)
            received[step] = moving
        shard_rows = jnp.stack([received[d] for d in range(owners)])
        blocks = shard_rows.reshape(slot_total, half_p, sample_count)
        full = jnp.einsum(
            "jps,sbk->jpbk", blocks, geno_blocks, preferred_element_type=jnp.float32
        )
        local_gradient = full[ring_slot, :, blk, :]
        split = local_gradient.reshape(cores, share, half_p, block_width)
        keep = lax.dynamic_index_in_dim(split, c, 0, keepdims=False)
        give = lax.dynamic_index_in_dim(split, 1 - c, 0, keepdims=False)
        own_gradient = keep + lax.ppermute(give, "sc", swap)
        own = shrink_soft(own, own_gradient, own_cutoff, own_active)
        if sweep + 1 < ITERS:
            own_bf = own.astype(jnp.bfloat16)
            other_bf = lax.ppermute(own_bf, "sc", swap)
            weight_bf = jnp.where(
                c == 0,
                jnp.concatenate([own_bf, other_bf], axis=0),
                jnp.concatenate([other_bf, own_bf], axis=0),
            )
    other_half = lax.ppermute(own, "sx", swap)
    mine = jnp.where(
        x == 0,
        jnp.concatenate([own, other_half], axis=1),
        jnp.concatenate([other_half, own], axis=1),
    )
    other_entries = lax.ppermute(mine, "sc", swap)
    return jnp.where(
        c == 0,
        jnp.concatenate([mine, other_entries], axis=0),
        jnp.concatenate([other_entries, mine], axis=0),
    )


def solution(mesh):
    snp_size, samp_size = mesh.devices.shape
    devices = mesh.devices.reshape(snp_size, 2, samp_size // 2)
    mesh = jax.sharding.Mesh(devices, ("snp", "sx", "sc"))
    samp = ("sx", "sc")
    in_specs = (
        P(samp, "snp"),
        P("snp", samp),
        P("snp", None, None),
        P("snp", None),
        P("snp"),
        P(),
        P(),
    )
    out_specs = P("snp", None, None)
    return jax.shard_map(
        per_device, mesh=mesh, in_specs=in_specs, out_specs=out_specs, check_vma=False
    )
```

```python
import jax
import jax.numpy as jnp
from jax import lax
from jax.sharding import PartitionSpec as P

ITERS = 2


step_scale = 0.3


def shrink_soft(current, gradient, cutoff, active):
    shifted = current + step_scale * gradient
    shrunk = jnp.sign(shifted) * jnp.maximum(jnp.abs(shifted) - cutoff, jnp.float32(0.0))
    return jnp.where(active[:, None, None], shrunk, jnp.float32(0.0))


def per_device(genotypes, responses, weights, pattern, entry_count, tile_slot, penalty):
    quarter = genotypes.shape[0]
    entries, tile_width, block_width = weights.shape
    block_count = genotypes.shape[1] // block_width
    own_rows = responses.shape[0]
    owners = lax.axis_size("snp")
    own_slots = own_rows // tile_width
    slot_total = owners * own_slots
    cells = slot_total * block_count
    halves = lax.axis_size("sx")
    cores = lax.axis_size("sc")
    half_p = tile_width // halves
    x = lax.axis_index("sx")
    c = lax.axis_index("sc")

    swap = [(0, 1), (1, 0)]
    geno_peer = lax.ppermute(genotypes, "sx", swap)
    geno = jnp.concatenate([genotypes, geno_peer], axis=0)
    sample_count = geno.shape[0]
    geno_blocks = geno.reshape(sample_count, block_count, block_width)
    resp4 = responses.reshape(own_slots, halves, half_p, quarter)
    resp_own = lax.dynamic_slice_in_dim(resp4, x, 1, 1)[:, 0]
    resp_peer = lax.ppermute(lax.dynamic_slice_in_dim(resp4, 1 - x, 1, 1)[:, 0], "sx", swap)
    resp = jnp.concatenate([resp_own, resp_peer], axis=2).reshape(
        own_slots * half_p, halves * quarter
    )

    blk = pattern[:, 0]
    tile = pattern[:, 1]
    tile_hot = tile[:, None] == jnp.arange(penalty.shape[0], dtype=jnp.int32)[None, :]
    slot_ids = jnp.sum(jnp.where(tile_hot, tile_slot[None, :], 0), axis=1)
    per_entry = jnp.sum(jnp.where(tile_hot, penalty[None, :], jnp.float32(0.0)), axis=1)
    cutoff = step_scale * per_entry[:, None, None]
    cell = slot_ids * block_count + blk
    cell_hot = (cell[:, None] == jnp.arange(cells, dtype=jnp.int32)[None, :]).astype(jnp.bfloat16)
    ring = list(range(0, owners, 2)) + list(range(owners - 1, 0, -2))
    ring_pos = [0] * owners
    for k, dev in enumerate(ring):
        ring_pos[dev] = k
    forward = [(ring[k], ring[(k + 1) % owners]) for k in range(owners)]
    backward = [(ring[k], ring[(k - 1) % owners]) for k in range(owners)]
    forward_steps = owners // 2
    ring_table = jnp.asarray(ring_pos, dtype=jnp.int32)
    ring_order = jnp.asarray(ring, dtype=jnp.int32)
    here = ring_table[lax.axis_index("snp")]
    rel_owner = (ring_table[slot_ids // own_slots] - here) % owners
    ring_slot = rel_owner * own_slots + slot_ids % own_slots
    active = jnp.arange(entries, dtype=jnp.int32) < entry_count[0]
    w_half = lax.dynamic_slice_in_dim(weights, x * half_p, half_p, 1)
    weight_bf = jnp.where(active[:, None, None], w_half, jnp.float32(0.0)).astype(jnp.bfloat16)
    share = entries // cores
    start = c * share
    own_active = lax.dynamic_slice_in_dim(active, start, share, 0)
    own_cutoff = lax.dynamic_slice_in_dim(cutoff, start, share, 0)
    own = jnp.where(
        own_active[:, None, None],
        lax.dynamic_slice_in_dim(w_half, start, share, 0),
        jnp.float32(0.0),
    )
    def ring_predict(dense):
        partial = jnp.einsum(
            "jbpk,sbk->jps", dense, geno_blocks, preferred_element_type=jnp.float32
        ).astype(jnp.bfloat16)
        partial = partial.reshape(owners, own_slots * half_p, sample_count)

        def owner_block(distance):
            owner = ring_order[(here + distance) % owners]
            return lax.dynamic_index_in_dim(partial, owner, 0, keepdims=False)

        ahead = lax.ppermute(owner_block(forward_steps), "snp", forward).astype(jnp.float32)
        for step in range(2, forward_steps + 1):
            carry = ahead + owner_block(forward_steps - step + 1).astype(jnp.float32)
            ahead = lax.ppermute(carry, "snp", forward)
        prediction = owner_block(0).astype(jnp.float32) + ahead
        behind_steps = owners - 1 - forward_steps
        if behind_steps > 0:
            behind = lax.ppermute(owner_block(-behind_steps), "snp", backward).astype(jnp.float32)
            for step in range(2, behind_steps + 1):
                carry = behind + owner_block(step - behind_steps - 1).astype(jnp.float32)
                behind = lax.ppermute(carry, "snp", backward)
            prediction = prediction + behind
        return prediction

    for sweep in range(ITERS):
        dense = jnp.einsum(
            "ec,epk->cpk", cell_hot, weight_bf, preferred_element_type=jnp.float32
        ).astype(jnp.bfloat16)
        dense = dense.reshape(slot_total, block_count, half_p, block_width)

        def predict(samples):
            count = samples.shape[0]
            partial = jnp.einsum(
                "jbpk,sbk->jps",
                dense,
                samples.reshape(count, block_count, block_width),
                preferred_element_type=jnp.float32,
            ).astype(jnp.bfloat16)
            partial = partial.reshape(owners, own_slots * half_p, count)
            gathered = lax.all_to_all(partial, "snp", 0, 0, tiled=False)
            return jnp.sum(gathered.astype(jnp.float32), axis=0)

        if sweep == 0:
            prediction = jnp.concatenate([predict(genotypes), predict(geno_peer)], axis=1)
        else:
            prediction = ring_predict(dense)
        residual = (resp - prediction).astype(jnp.bfloat16)
        received = {0: residual}
        moving = residual
        for step in range(1, forward_steps + 1):
            moving = lax.ppermute(moving, "snp", forward)
            received[owners - step] = moving
        moving = residual
        for step in range(1, owners - forward_steps):
            moving = lax.ppermute(moving, "snp", backward)
            received[step] = moving
        shard_rows = jnp.stack([received[d] for d in range(owners)])
        blocks = shard_rows.reshape(slot_total, half_p, sample_count)
        full = jnp.einsum(
            "jps,sbk->jpbk", blocks, geno_blocks, preferred_element_type=jnp.float32
        )
        local_gradient = full[ring_slot, :, blk, :]
        split = local_gradient.reshape(cores, share, half_p, block_width)
        keep = lax.dynamic_index_in_dim(split, c, 0, keepdims=False)
        give = lax.dynamic_index_in_dim(split, 1 - c, 0, keepdims=False)
        own_gradient = keep + lax.ppermute(give, "sc", swap)
        own = shrink_soft(own, own_gradient, own_cutoff, own_active)
        if sweep + 1 < ITERS:
            own_bf = own.astype(jnp.bfloat16)
            other_bf = lax.ppermute(own_bf, "sc", swap)
            weight_bf = jnp.where(
                c == 0,
                jnp.concatenate([own_bf, other_bf], axis=0),
                jnp.concatenate([other_bf, own_bf], axis=0),
            )
    other_half = lax.ppermute(own, "sx", swap)
    mine = jnp.where(
        x == 0,
        jnp.concatenate([own, other_half], axis=1),
        jnp.concatenate([other_half, own], axis=1),
    )
    other_entries = lax.ppermute(mine, "sc", swap)
    return jnp.where(
        c == 0,
        jnp.concatenate([mine, other_entries], axis=0),
        jnp.concatenate([other_entries, mine], axis=0),
    )


def solution(mesh):
    snp_size, samp_size = mesh.devices.shape
    devices = mesh.devices.reshape(snp_size, 2, samp_size // 2)
    mesh = jax.sharding.Mesh(devices, ("snp", "sx", "sc"))
    samp = ("sx", "sc")
    in_specs = (
        P(samp, "snp"),
        P("snp", samp),
        P("snp", None, None),
        P("snp", None),
        P("snp"),
        P(),
        P(),
    )
    out_specs = P("snp", None, None)
    return jax.shard_map(
        per_device, mesh=mesh, in_specs=in_specs, out_specs=out_specs, check_vma=False
    )
```

```python
import jax
import jax.numpy as jnp
from jax import lax
from jax.sharding import PartitionSpec as P

ITERS = 2


step_scale = 0.3


def shrink_soft(current, gradient, cutoff, active):
    shifted = current + step_scale * gradient
    shrunk = jnp.sign(shifted) * jnp.maximum(jnp.abs(shifted) - cutoff, jnp.float32(0.0))
    return jnp.where(active[:, None, None], shrunk, jnp.float32(0.0))


def per_device(genotypes, responses, weights, pattern, entry_count, tile_slot, penalty):
    quarter = genotypes.shape[0]
    entries, tile_width, block_width = weights.shape
    block_count = genotypes.shape[1] // block_width
    own_rows = responses.shape[0]
    owners = lax.axis_size("snp")
    own_slots = own_rows // tile_width
    slot_total = owners * own_slots
    cells = slot_total * block_count
    halves = lax.axis_size("sx")
    cores = lax.axis_size("sc")
    half_p = tile_width // halves
    x = lax.axis_index("sx")
    c = lax.axis_index("sc")

    swap = [(0, 1), (1, 0)]
    geno_peer = lax.ppermute(genotypes, "sx", swap)
    geno = jnp.concatenate([genotypes, geno_peer], axis=0)
    sample_count = geno.shape[0]
    geno_blocks = geno.reshape(sample_count, block_count, block_width)
    resp4 = responses.reshape(own_slots, halves, half_p, quarter)
    resp_own = lax.dynamic_slice_in_dim(resp4, x, 1, 1)[:, 0]
    resp_peer = lax.ppermute(lax.dynamic_slice_in_dim(resp4, 1 - x, 1, 1)[:, 0], "sx", swap)
    resp = jnp.concatenate([resp_own, resp_peer], axis=2).reshape(
        own_slots * half_p, halves * quarter
    )

    blk = pattern[:, 0]
    tile = pattern[:, 1]
    tile_hot = tile[:, None] == jnp.arange(penalty.shape[0], dtype=jnp.int32)[None, :]
    slot_ids = jnp.sum(jnp.where(tile_hot, tile_slot[None, :], 0), axis=1)
    per_entry = jnp.sum(jnp.where(tile_hot, penalty[None, :], jnp.float32(0.0)), axis=1)
    cutoff = step_scale * per_entry[:, None, None]
    cell = slot_ids * block_count + blk
    cell_hot = (cell[:, None] == jnp.arange(cells, dtype=jnp.int32)[None, :]).astype(jnp.bfloat16)
    ring = list(range(0, owners, 2)) + list(range(owners - 1, 0, -2))
    ring_pos = [0] * owners
    for k, dev in enumerate(ring):
        ring_pos[dev] = k
    forward = [(ring[k], ring[(k + 1) % owners]) for k in range(owners)]
    backward = [(ring[k], ring[(k - 1) % owners]) for k in range(owners)]
    forward_steps = owners // 2
    ring_table = jnp.asarray(ring_pos, dtype=jnp.int32)
    here = ring_table[lax.axis_index("snp")]
    rel_owner = (ring_table[slot_ids // own_slots] - here) % owners
    ring_slot = rel_owner * own_slots + slot_ids % own_slots
    active = jnp.arange(entries, dtype=jnp.int32) < entry_count[0]
    w_half = lax.dynamic_slice_in_dim(weights, x * half_p, half_p, 1)
    weight_bf = jnp.where(active[:, None, None], w_half, jnp.float32(0.0)).astype(jnp.bfloat16)
    share = entries // cores
    start = c * share
    own_active = lax.dynamic_slice_in_dim(active, start, share, 0)
    own_cutoff = lax.dynamic_slice_in_dim(cutoff, start, share, 0)
    own = jnp.where(
        own_active[:, None, None],
        lax.dynamic_slice_in_dim(w_half, start, share, 0),
        jnp.float32(0.0),
    )
    for sweep in range(ITERS):
        dense = jnp.einsum(
            "ec,epk->cpk", cell_hot, weight_bf, preferred_element_type=jnp.float32
        ).astype(jnp.bfloat16)
        dense = dense.reshape(slot_total, block_count, half_p, block_width)

        def predict(samples):
            count = samples.shape[0]
            partial = jnp.einsum(
                "jbpk,sbk->jps",
                dense,
                samples.reshape(count, block_count, block_width),
                preferred_element_type=jnp.float32,
            ).astype(jnp.bfloat16)
            partial = partial.reshape(owners, own_slots * half_p, count)
            gathered = lax.all_to_all(partial, "snp", 0, 0, tiled=False)
            return jnp.sum(gathered.astype(jnp.float32), axis=0)

        if sweep == 0:
            prediction = jnp.concatenate([predict(genotypes), predict(geno_peer)], axis=1)
        else:
            prediction = predict(geno)
        residual = (resp - prediction).astype(jnp.bfloat16)
        received = {0: residual}
        full_steps = owners - 1 - forward_steps
        split_far = owners % 2 == 0 and full_steps > 0
        ahead_moving = residual
        behind_moving = residual
        for step in range(1, full_steps + 1):
            ahead_moving = lax.ppermute(ahead_moving, "snp", forward)
            received[owners - step] = ahead_moving
            behind_moving = lax.ppermute(behind_moving, "snp", backward)
            received[step] = behind_moving
        if split_far:
            half_rows = residual.shape[0] // 2
            first = lax.ppermute(ahead_moving[:half_rows], "snp", forward)
            second = lax.ppermute(behind_moving[half_rows:], "snp", backward)
            received[forward_steps] = jnp.concatenate([first, second], axis=0)
        else:
            for step in range(full_steps + 1, forward_steps + 1):
                ahead_moving = lax.ppermute(ahead_moving, "snp", forward)
                received[owners - step] = ahead_moving
        shard_rows = jnp.stack([received[d] for d in range(owners)])
        blocks = shard_rows.reshape(slot_total, half_p, sample_count)
        full = jnp.einsum(
            "jps,sbk->jpbk", blocks, geno_blocks, preferred_element_type=jnp.float32
        )
        local_gradient = full[ring_slot, :, blk, :]
        split = local_gradient.reshape(cores, share, half_p, block_width)
        keep = lax.dynamic_index_in_dim(split, c, 0, keepdims=False)
        give = lax.dynamic_index_in_dim(split, 1 - c, 0, keepdims=False)
        own_gradient = keep + lax.ppermute(give, "sc", swap)
        own = shrink_soft(own, own_gradient, own_cutoff, own_active)
        if sweep + 1 < ITERS:
            own_bf = own.astype(jnp.bfloat16)
            other_bf = lax.ppermute(own_bf, "sc", swap)
            weight_bf = jnp.where(
                c == 0,
                jnp.concatenate([own_bf, other_bf], axis=0),
                jnp.concatenate([other_bf, own_bf], axis=0),
            )
    other_half = lax.ppermute(own, "sx", swap)
    mine = jnp.where(
        x == 0,
        jnp.concatenate([own, other_half], axis=1),
        jnp.concatenate([other_half, own], axis=1),
    )
    other_entries = lax.ppermute(mine, "sc", swap)
    return jnp.where(
        c == 0,
        jnp.concatenate([mine, other_entries], axis=0),
        jnp.concatenate([other_entries, mine], axis=0),
    )


def solution(mesh):
    snp_size, samp_size = mesh.devices.shape
    devices = mesh.devices.reshape(snp_size, 2, samp_size // 2)
    mesh = jax.sharding.Mesh(devices, ("snp", "sx", "sc"))
    samp = ("sx", "sc")
    in_specs = (
        P(samp, "snp"),
        P("snp", samp),
        P("snp", None, None),
        P("snp", None),
        P("snp"),
        P(),
        P(),
    )
    out_specs = P("snp", None, None)
    return jax.shard_map(
        per_device, mesh=mesh, in_specs=in_specs, out_specs=out_specs, check_vma=False
    )
```

```python
import jax
import jax.numpy as jnp
from jax import lax
from jax.sharding import PartitionSpec as P

ITERS = 2


step_scale = 0.3


def shrink_soft(current, gradient, cutoff, active):
    shifted = current + step_scale * gradient
    shrunk = jnp.sign(shifted) * jnp.maximum(jnp.abs(shifted) - cutoff, jnp.float32(0.0))
    return jnp.where(active[:, None, None], shrunk, jnp.float32(0.0))


def per_device(genotypes, responses, weights, pattern, entry_count, tile_slot, penalty):
    quarter = genotypes.shape[0]
    entries, tile_width, block_width = weights.shape
    block_count = genotypes.shape[1] // block_width
    own_rows = responses.shape[0]
    owners = lax.axis_size("snp")
    own_slots = own_rows // tile_width
    slot_total = owners * own_slots
    cells = slot_total * block_count
    halves = lax.axis_size("sx")
    cores = lax.axis_size("sc")
    half_p = tile_width // halves
    x = lax.axis_index("sx")
    c = lax.axis_index("sc")

    swap = [(0, 1), (1, 0)]
    geno_peer = lax.ppermute(genotypes, "sx", swap)
    geno = jnp.concatenate([genotypes, geno_peer], axis=0)
    sample_count = geno.shape[0]
    geno_blocks = geno.reshape(sample_count, block_count, block_width)
    resp4 = responses.reshape(own_slots, halves, half_p, quarter)
    resp_own = lax.dynamic_slice_in_dim(resp4, x, 1, 1)[:, 0]
    resp_peer = lax.ppermute(lax.dynamic_slice_in_dim(resp4, 1 - x, 1, 1)[:, 0], "sx", swap)
    resp = jnp.concatenate([resp_own, resp_peer], axis=2).reshape(
        own_slots * half_p, halves * quarter
    )

    blk = pattern[:, 0]
    tile = pattern[:, 1]
    tile_hot = tile[:, None] == jnp.arange(penalty.shape[0], dtype=jnp.int32)[None, :]
    slot_ids = jnp.sum(jnp.where(tile_hot, tile_slot[None, :], 0), axis=1)
    per_entry = jnp.sum(jnp.where(tile_hot, penalty[None, :], jnp.float32(0.0)), axis=1)
    cutoff = step_scale * per_entry[:, None, None]
    cell = slot_ids * block_count + blk
    cell_hot = (cell[:, None] == jnp.arange(cells, dtype=jnp.int32)[None, :]).astype(jnp.bfloat16)
    ring = list(range(0, owners, 2)) + list(range(owners - 1, 0, -2))
    ring_pos = [0] * owners
    for k, dev in enumerate(ring):
        ring_pos[dev] = k
    forward = [(ring[k], ring[(k + 1) % owners]) for k in range(owners)]
    backward = [(ring[k], ring[(k - 1) % owners]) for k in range(owners)]
    forward_steps = owners // 2
    ring_table = jnp.asarray(ring_pos, dtype=jnp.int32)
    here = ring_table[lax.axis_index("snp")]
    rel_owner = (ring_table[slot_ids // own_slots] - here) % owners
    ring_slot = rel_owner * own_slots + slot_ids % own_slots
    active = jnp.arange(entries, dtype=jnp.int32) < entry_count[0]
    w_half = lax.dynamic_slice_in_dim(weights, x * half_p, half_p, 1)
    weight_bf = jnp.where(active[:, None, None], w_half, jnp.float32(0.0)).astype(jnp.bfloat16)
    share = entries // cores
    start = c * share
    own_active = lax.dynamic_slice_in_dim(active, start, share, 0)
    own_cutoff = lax.dynamic_slice_in_dim(cutoff, start, share, 0)
    own = jnp.where(
        own_active[:, None, None],
        lax.dynamic_slice_in_dim(w_half, start, share, 0),
        jnp.float32(0.0),
    )
    for sweep in range(ITERS):
        dense = jnp.einsum(
            "ec,epk->cpk", cell_hot, weight_bf, preferred_element_type=jnp.float32
        ).astype(jnp.bfloat16)
        dense = dense.reshape(slot_total, block_count, half_p, block_width)

        def predict(samples):
            count = samples.shape[0]
            partial = jnp.einsum(
                "jbpk,sbk->jps",
                dense,
                samples.reshape(count, block_count, block_width),
                preferred_element_type=jnp.float32,
            ).astype(jnp.bfloat16)
            partial = partial.reshape(owners, own_slots * half_p, count)
            gathered = lax.all_to_all(partial, "snp", 0, 0, tiled=False)
            return jnp.sum(gathered.astype(jnp.float32), axis=0)

        def ring_gather(residual):
            received = {0: residual}
            moving = residual
            for step in range(1, forward_steps + 1):
                moving = lax.ppermute(moving, "snp", forward)
                received[owners - step] = moving
            moving = residual
            for step in range(1, owners - forward_steps):
                moving = lax.ppermute(moving, "snp", backward)
                received[step] = moving
            return jnp.stack([received[d] for d in range(owners)])

        if sweep == 0:
            first = (resp[:, :quarter] - predict(genotypes)).astype(jnp.bfloat16)
            first_rows = ring_gather(first)
            second = (resp[:, quarter:] - predict(geno_peer)).astype(jnp.bfloat16)
            shard_rows = jnp.concatenate([first_rows, ring_gather(second)], axis=2)
        else:
            residual = (resp - predict(geno)).astype(jnp.bfloat16)
            shard_rows = ring_gather(residual)
        blocks = shard_rows.reshape(slot_total, half_p, sample_count)
        full = jnp.einsum(
            "jps,sbk->jpbk", blocks, geno_blocks, preferred_element_type=jnp.float32
        )
        local_gradient = full[ring_slot, :, blk, :]
        split = local_gradient.reshape(cores, share, half_p, block_width)
        keep = lax.dynamic_index_in_dim(split, c, 0, keepdims=False)
        give = lax.dynamic_index_in_dim(split, 1 - c, 0, keepdims=False)
        own_gradient = keep + lax.ppermute(give, "sc", swap)
        own = shrink_soft(own, own_gradient, own_cutoff, own_active)
        if sweep + 1 < ITERS:
            own_bf = own.astype(jnp.bfloat16)
            other_bf = lax.ppermute(own_bf, "sc", swap)
            weight_bf = jnp.where(
                c == 0,
                jnp.concatenate([own_bf, other_bf], axis=0),
                jnp.concatenate([other_bf, own_bf], axis=0),
            )
    other_half = lax.ppermute(own, "sx", swap)
    mine = jnp.where(
        x == 0,
        jnp.concatenate([own, other_half], axis=1),
        jnp.concatenate([other_half, own], axis=1),
    )
    other_entries = lax.ppermute(mine, "sc", swap)
    return jnp.where(
        c == 0,
        jnp.concatenate([mine, other_entries], axis=0),
        jnp.concatenate([other_entries, mine], axis=0),
    )


def solution(mesh):
    snp_size, samp_size = mesh.devices.shape
    devices = mesh.devices.reshape(snp_size, 2, samp_size // 2)
    mesh = jax.sharding.Mesh(devices, ("snp", "sx", "sc"))
    samp = ("sx", "sc")
    in_specs = (
        P(samp, "snp"),
        P("snp", samp),
        P("snp", None, None),
        P("snp", None),
        P("snp"),
        P(),
        P(),
    )
    out_specs = P("snp", None, None)
    return jax.shard_map(
        per_device, mesh=mesh, in_specs=in_specs, out_specs=out_specs, check_vma=False
    )
```

```python
import jax
import jax.numpy as jnp
from jax import lax
from jax.sharding import PartitionSpec as P

ITERS = 2


step_scale = 0.3


def shrink_soft(current, gradient, cutoff, active):
    shifted = current + step_scale * gradient
    shrunk = jnp.sign(shifted) * jnp.maximum(jnp.abs(shifted) - cutoff, jnp.float32(0.0))
    return jnp.where(active[:, None, None], shrunk, jnp.float32(0.0))


def per_device(genotypes, responses, weights, pattern, entry_count, tile_slot, penalty):
    quarter = genotypes.shape[0]
    entries, tile_width, block_width = weights.shape
    block_count = genotypes.shape[1] // block_width
    own_rows = responses.shape[0]
    owners = lax.axis_size("snp")
    own_slots = own_rows // tile_width
    slot_total = owners * own_slots
    cells = slot_total * block_count
    halves = lax.axis_size("sx")
    cores = lax.axis_size("sc")
    half_p = tile_width // halves
    x = lax.axis_index("sx")
    c = lax.axis_index("sc")

    swap = [(0, 1), (1, 0)]
    geno_peer = lax.ppermute(genotypes, "sx", swap)
    geno = jnp.concatenate([genotypes, geno_peer], axis=0)
    sample_count = geno.shape[0]
    geno_blocks = geno.reshape(sample_count, block_count, block_width)
    resp4 = responses.reshape(own_slots, halves, half_p, quarter)
    resp_own = lax.dynamic_slice_in_dim(resp4, x, 1, 1)[:, 0]
    resp_peer = lax.ppermute(lax.dynamic_slice_in_dim(resp4, 1 - x, 1, 1)[:, 0], "sx", swap)
    resp = jnp.concatenate([resp_own, resp_peer], axis=2).reshape(
        own_slots * half_p, halves * quarter
    )

    blk = pattern[:, 0]
    tile = pattern[:, 1]
    tile_hot = tile[:, None] == jnp.arange(penalty.shape[0], dtype=jnp.int32)[None, :]
    slot_ids = jnp.sum(jnp.where(tile_hot, tile_slot[None, :], 0), axis=1)
    per_entry = jnp.sum(jnp.where(tile_hot, penalty[None, :], jnp.float32(0.0)), axis=1)
    cutoff = step_scale * per_entry[:, None, None]
    cell = slot_ids * block_count + blk
    cell_hot = (cell[:, None] == jnp.arange(cells, dtype=jnp.int32)[None, :]).astype(jnp.bfloat16)
    ring = list(range(0, owners, 2)) + list(range(owners - 1, 0, -2))
    ring_pos = [0] * owners
    for k, dev in enumerate(ring):
        ring_pos[dev] = k
    forward = [(ring[k], ring[(k + 1) % owners]) for k in range(owners)]
    backward = [(ring[k], ring[(k - 1) % owners]) for k in range(owners)]
    forward_steps = owners // 2
    ring_table = jnp.asarray(ring_pos, dtype=jnp.int32)
    here = ring_table[lax.axis_index("snp")]
    rel_owner = (ring_table[slot_ids // own_slots] - here) % owners
    ring_slot = rel_owner * own_slots + slot_ids % own_slots
    active = jnp.arange(entries, dtype=jnp.int32) < entry_count[0]
    w_half = lax.dynamic_slice_in_dim(weights, x * half_p, half_p, 1)
    weight_bf = jnp.where(active[:, None, None], w_half, jnp.float32(0.0)).astype(jnp.bfloat16)
    share = entries // cores
    start = c * share
    own_active = lax.dynamic_slice_in_dim(active, start, share, 0)
    own_cutoff = lax.dynamic_slice_in_dim(cutoff, start, share, 0)
    own = jnp.where(
        own_active[:, None, None],
        lax.dynamic_slice_in_dim(w_half, start, share, 0),
        jnp.float32(0.0),
    )
    for sweep in range(ITERS):
        dense = jnp.einsum(
            "ec,epk->cpk", cell_hot, weight_bf, preferred_element_type=jnp.float32
        ).astype(jnp.bfloat16)
        dense = dense.reshape(slot_total, block_count, half_p, block_width)

        def predict(samples):
            count = samples.shape[0]
            partial = jnp.einsum(
                "jbpk,sbk->jps",
                dense,
                samples.reshape(count, block_count, block_width),
                preferred_element_type=jnp.float32,
            ).astype(jnp.bfloat16)
            partial = partial.reshape(owners, own_slots * half_p, count)
            gathered = lax.all_to_all(partial, "snp", 0, 0, tiled=False)
            return jnp.sum(gathered.astype(jnp.float32), axis=0)

        if sweep == 0:
            prediction = jnp.concatenate([predict(genotypes), predict(geno_peer)], axis=1)
        else:
            prediction = predict(geno)
        residual = (resp - prediction).astype(jnp.bfloat16)
        received = {0: residual}
        moving = residual
        for step in range(1, forward_steps + 1):
            moving = lax.ppermute(moving, "snp", forward)
            received[owners - step] = moving
        moving = residual
        for step in range(1, owners - forward_steps):
            moving = lax.ppermute(moving, "snp", backward)
            received[step] = moving
        shard_rows = jnp.stack([received[d] for d in range(owners)])
        blocks = shard_rows.reshape(slot_total, half_p, sample_count)
        full = jnp.einsum(
            "jps,sbk->jpbk", blocks, geno_blocks, preferred_element_type=jnp.float32
        )
        local_gradient = full[ring_slot, :, blk, :]
        split = local_gradient.reshape(cores, share, half_p, block_width)
        keep = lax.dynamic_index_in_dim(split, c, 0, keepdims=False)
        give = lax.dynamic_index_in_dim(split, 1 - c, 0, keepdims=False)
        own_gradient = keep + lax.ppermute(give, "sc", swap)
        own = shrink_soft(own, own_gradient, own_cutoff, own_active)
        if sweep + 1 < ITERS:
            own_bf = own.astype(jnp.bfloat16)
            other_bf = lax.ppermute(own_bf, "sc", swap)
            weight_bf = jnp.where(
                c == 0,
                jnp.concatenate([own_bf, other_bf], axis=0),
                jnp.concatenate([other_bf, own_bf], axis=0),
            )
    other_half = lax.ppermute(own, "sx", swap)
    core_own = lax.ppermute(own, "sc", swap)
    core_other = lax.ppermute(other_half, "sc", swap)
    mine = jnp.where(
        x == 0,
        jnp.concatenate([own, other_half], axis=1),
        jnp.concatenate([other_half, own], axis=1),
    )
    other_entries = jnp.where(
        x == 0,
        jnp.concatenate([core_own, core_other], axis=1),
        jnp.concatenate([core_other, core_own], axis=1),
    )
    return jnp.where(
        c == 0,
        jnp.concatenate([mine, other_entries], axis=0),
        jnp.concatenate([other_entries, mine], axis=0),
    )


def solution(mesh):
    snp_size, samp_size = mesh.devices.shape
    devices = mesh.devices.reshape(snp_size, 2, samp_size // 2)
    mesh = jax.sharding.Mesh(devices, ("snp", "sx", "sc"))
    samp = ("sx", "sc")
    in_specs = (
        P(samp, "snp"),
        P("snp", samp),
        P("snp", None, None),
        P("snp", None),
        P("snp"),
        P(),
        P(),
    )
    out_specs = P("snp", None, None)
    return jax.shard_map(
        per_device, mesh=mesh, in_specs=in_specs, out_specs=out_specs, check_vma=False
    )
```

```python
import jax
import jax.numpy as jnp
from jax import lax
from jax.sharding import PartitionSpec as P

ITERS = 2


step_scale = 0.3


def shrink_soft(current, gradient, cutoff, active):
    shifted = current + step_scale * gradient
    shrunk = jnp.sign(shifted) * jnp.maximum(jnp.abs(shifted) - cutoff, jnp.float32(0.0))
    return jnp.where(active[:, None, None], shrunk, jnp.float32(0.0))


def per_device(genotypes, responses, weights, pattern, entry_count, tile_slot, penalty):
    quarter = genotypes.shape[0]
    entries, tile_width, block_width = weights.shape
    block_count = genotypes.shape[1] // block_width
    own_rows = responses.shape[0]
    owners = lax.axis_size("snp")
    own_slots = own_rows // tile_width
    slot_total = owners * own_slots
    cells = slot_total * block_count
    halves = lax.axis_size("sx")
    cores = lax.axis_size("sc")
    half_p = tile_width // halves
    x = lax.axis_index("sx")
    c = lax.axis_index("sc")

    swap = [(0, 1), (1, 0)]
    geno_peer = lax.ppermute(genotypes, "sx", swap)
    geno = jnp.concatenate([genotypes, geno_peer], axis=0)
    sample_count = geno.shape[0]
    geno_blocks = geno.reshape(sample_count, block_count, block_width)
    resp4 = responses.reshape(own_slots, halves, half_p, quarter)
    resp_own = lax.dynamic_slice_in_dim(resp4, x, 1, 1)[:, 0]
    resp_peer = lax.ppermute(lax.dynamic_slice_in_dim(resp4, 1 - x, 1, 1)[:, 0], "sx", swap)
    resp = jnp.concatenate([resp_own, resp_peer], axis=2).reshape(
        own_slots * half_p, halves * quarter
    )

    blk = pattern[:, 0]
    tile = pattern[:, 1]
    tile_hot = tile[:, None] == jnp.arange(penalty.shape[0], dtype=jnp.int32)[None, :]
    slot_ids = jnp.sum(jnp.where(tile_hot, tile_slot[None, :], 0), axis=1)
    per_entry = jnp.sum(jnp.where(tile_hot, penalty[None, :], jnp.float32(0.0)), axis=1)
    cutoff = step_scale * per_entry[:, None, None]
    cell = slot_ids * block_count + blk
    cell_hot = (cell[:, None] == jnp.arange(cells, dtype=jnp.int32)[None, :]).astype(jnp.bfloat16)
    ring = list(range(0, owners, 2)) + list(range(owners - 1, 0, -2))
    ring_pos = [0] * owners
    for k, dev in enumerate(ring):
        ring_pos[dev] = k
    forward = [(ring[k], ring[(k + 1) % owners]) for k in range(owners)]
    backward = [(ring[k], ring[(k - 1) % owners]) for k in range(owners)]
    forward_steps = owners // 2
    ring_table = jnp.asarray(ring_pos, dtype=jnp.int32)
    here = ring_table[lax.axis_index("snp")]
    rel_owner = (ring_table[slot_ids // own_slots] - here) % owners
    ring_slot = rel_owner * own_slots + slot_ids % own_slots
    active = jnp.arange(entries, dtype=jnp.int32) < entry_count[0]
    w_half = lax.dynamic_slice_in_dim(weights, x * half_p, half_p, 1)
    weight_bf = jnp.where(active[:, None, None], w_half, jnp.float32(0.0)).astype(jnp.bfloat16)
    share = entries // cores
    start = c * share
    own_active = lax.dynamic_slice_in_dim(active, start, share, 0)
    own_cutoff = lax.dynamic_slice_in_dim(cutoff, start, share, 0)
    own = jnp.where(
        own_active[:, None, None],
        lax.dynamic_slice_in_dim(w_half, start, share, 0),
        jnp.float32(0.0),
    )
    for sweep in range(ITERS):
        dense = jnp.einsum(
            "ec,epk->cpk", cell_hot, weight_bf, preferred_element_type=jnp.float32
        ).astype(jnp.bfloat16)
        dense = dense.reshape(slot_total, block_count, half_p, block_width)

        def predict(samples):
            count = samples.shape[0]
            partial = jnp.einsum(
                "jbpk,sbk->jps",
                dense,
                samples.reshape(count, block_count, block_width),
                preferred_element_type=jnp.float32,
            ).astype(jnp.bfloat16)
            partial = partial.reshape(owners, own_slots * half_p, count)
            gathered = lax.all_to_all(partial, "snp", 0, 0, tiled=False)
            return jnp.sum(gathered.astype(jnp.float32), axis=0)

        if sweep == 0:
            prediction = jnp.concatenate([predict(genotypes), predict(geno_peer)], axis=1)
        else:
            prediction = predict(geno)
        residual = (resp - prediction).astype(jnp.bfloat16)
        received = {0: residual}
        moving = residual
        for step in range(1, forward_steps + 1):
            moving = lax.ppermute(moving, "snp", forward)
            received[owners - step] = moving
        moving = residual
        for step in range(1, owners - forward_steps):
            moving = lax.ppermute(moving, "snp", backward)
            received[step] = moving
        shard_rows = jnp.stack([received[d] for d in range(owners)])
        blocks = shard_rows.reshape(slot_total, half_p, sample_count)
        full = jnp.einsum(
            "jps,sbk->jpbk", blocks, geno_blocks, preferred_element_type=jnp.float32
        )
        local_gradient = full[ring_slot, :, blk, :]
        split = local_gradient.reshape(cores, share, half_p, block_width)
        keep = lax.dynamic_index_in_dim(split, c, 0, keepdims=False)
        give = lax.dynamic_index_in_dim(split, 1 - c, 0, keepdims=False)
        own_gradient = keep + lax.ppermute(give, "sc", swap)
        own = shrink_soft(own, own_gradient, own_cutoff, own_active)
        if sweep + 1 < ITERS:
            own_bf = own.astype(jnp.bfloat16)
            other_bf = lax.ppermute(own_bf, "sc", swap)
            weight_bf = jnp.where(
                c == 0,
                jnp.concatenate([own_bf, other_bf], axis=0),
                jnp.concatenate([other_bf, own_bf], axis=0),
            )
    other_half = lax.ppermute(own, "sx", swap)
    core_own = lax.ppermute(own, "sc", swap)
    core_other = lax.ppermute(other_half, "sc", swap)
    result = jnp.zeros(weights.shape, jnp.float32)
    zero = jnp.int32(0)
    other_start = (1 - c) * share
    result = lax.dynamic_update_slice(result, own, (start, x * half_p, zero))
    result = lax.dynamic_update_slice(result, other_half, (start, (1 - x) * half_p, zero))
    result = lax.dynamic_update_slice(result, core_own, (other_start, x * half_p, zero))
    return lax.dynamic_update_slice(result, core_other, (other_start, (1 - x) * half_p, zero))


def solution(mesh):
    snp_size, samp_size = mesh.devices.shape
    devices = mesh.devices.reshape(snp_size, 2, samp_size // 2)
    mesh = jax.sharding.Mesh(devices, ("snp", "sx", "sc"))
    samp = ("sx", "sc")
    in_specs = (
        P(samp, "snp"),
        P("snp", samp),
        P("snp", None, None),
        P("snp", None),
        P("snp"),
        P(),
        P(),
    )
    out_specs = P("snp", None, None)
    return jax.shard_map(
        per_device, mesh=mesh, in_specs=in_specs, out_specs=out_specs, check_vma=False
    )
```

```python
import jax
import jax.numpy as jnp
from jax import lax
from jax.sharding import PartitionSpec as P

ITERS = 2


step_scale = 0.3


def shrink_soft(current, gradient, cutoff, active):
    shifted = current + step_scale * gradient
    shrunk = jnp.sign(shifted) * jnp.maximum(jnp.abs(shifted) - cutoff, jnp.float32(0.0))
    return jnp.where(active[:, None, None], shrunk, jnp.float32(0.0))


def per_device(genotypes, responses, weights, pattern, entry_count, tile_slot, penalty):
    quarter = genotypes.shape[0]
    entries, tile_width, block_width = weights.shape
    block_count = genotypes.shape[1] // block_width
    own_rows = responses.shape[0]
    owners = lax.axis_size("snp")
    own_slots = own_rows // tile_width
    slot_total = owners * own_slots
    cells = slot_total * block_count
    halves = lax.axis_size("sx")
    cores = lax.axis_size("sc")
    half_p = tile_width // halves
    x = lax.axis_index("sx")
    c = lax.axis_index("sc")

    swap = [(0, 1), (1, 0)]
    geno_peer = lax.ppermute(genotypes, "sx", swap)
    geno = jnp.concatenate([genotypes, geno_peer], axis=0)
    sample_count = geno.shape[0]
    geno_blocks = geno.reshape(sample_count, block_count, block_width)
    resp4 = responses.reshape(own_slots, halves, half_p, quarter)
    resp_own = lax.dynamic_slice_in_dim(resp4, x, 1, 1)[:, 0]
    resp_peer = lax.ppermute(lax.dynamic_slice_in_dim(resp4, 1 - x, 1, 1)[:, 0], "sx", swap)
    resp = jnp.concatenate([resp_own, resp_peer], axis=2).reshape(
        own_slots * half_p, halves * quarter
    )

    blk = pattern[:, 0]
    tile = pattern[:, 1]
    tile_hot = tile[:, None] == jnp.arange(penalty.shape[0], dtype=jnp.int32)[None, :]
    slot_ids = jnp.sum(jnp.where(tile_hot, tile_slot[None, :], 0), axis=1)
    per_entry = jnp.sum(jnp.where(tile_hot, penalty[None, :], jnp.float32(0.0)), axis=1)
    cutoff = step_scale * per_entry[:, None, None]
    cell = slot_ids * block_count + blk
    cell_hot = (cell[:, None] == jnp.arange(cells, dtype=jnp.int32)[None, :]).astype(jnp.bfloat16)
    ring = list(range(0, owners, 2)) + list(range(owners - 1, 0, -2))
    ring_pos = [0] * owners
    for k, dev in enumerate(ring):
        ring_pos[dev] = k
    forward = [(ring[k], ring[(k + 1) % owners]) for k in range(owners)]
    backward = [(ring[k], ring[(k - 1) % owners]) for k in range(owners)]
    forward_steps = owners // 2
    ring_table = jnp.asarray(ring_pos, dtype=jnp.int32)
    here = ring_table[lax.axis_index("snp")]
    rel_owner = (ring_table[slot_ids // own_slots] - here) % owners
    ring_slot = rel_owner * own_slots + slot_ids % own_slots
    active = jnp.arange(entries, dtype=jnp.int32) < entry_count[0]
    w_half = lax.dynamic_slice_in_dim(weights, x * half_p, half_p, 1)
    weight_bf = jnp.where(active[:, None, None], w_half, jnp.float32(0.0)).astype(jnp.bfloat16)
    share = entries // cores
    start = c * share
    own_active = lax.dynamic_slice_in_dim(active, start, share, 0)
    own_cutoff = lax.dynamic_slice_in_dim(cutoff, start, share, 0)
    own = jnp.where(
        own_active[:, None, None],
        lax.dynamic_slice_in_dim(w_half, start, share, 0),
        jnp.float32(0.0),
    )
    for sweep in range(ITERS):
        dense = jnp.einsum(
            "ec,epk->cpk", cell_hot, weight_bf, preferred_element_type=jnp.float32
        ).astype(jnp.bfloat16)
        dense = dense.reshape(slot_total, block_count, half_p, block_width)

        def predict(samples):
            count = samples.shape[0]
            partial = jnp.einsum(
                "jbpk,sbk->jps",
                dense,
                samples.reshape(count, block_count, block_width),
                preferred_element_type=jnp.float32,
            ).astype(jnp.bfloat16)
            partial = partial.reshape(owners, own_slots * half_p, count)
            gathered = lax.all_to_all(partial, "snp", 0, 0, tiled=False)
            return jnp.sum(gathered.astype(jnp.float32), axis=0)

        if sweep == 0:
            prediction = jnp.concatenate([predict(genotypes), predict(geno_peer)], axis=1)
        else:
            prediction = predict(geno)
        residual = (resp - prediction).astype(jnp.bfloat16)
        received = {0: residual}
        moving = residual
        for step in range(1, forward_steps + 1):
            moving = lax.ppermute(moving, "snp", forward)
            received[owners - step] = moving
        moving = residual
        for step in range(1, owners - forward_steps):
            moving = lax.ppermute(moving, "snp", backward)
            received[step] = moving
        shard_rows = jnp.stack([received[d] for d in range(owners)])
        blocks = shard_rows.reshape(slot_total, half_p, sample_count)
        full = jnp.einsum(
            "jps,sbk->jpbk", blocks, geno_blocks, preferred_element_type=jnp.float32
        )
        local_gradient = full[ring_slot, :, blk, :]
        split = local_gradient.reshape(cores, share, half_p, block_width)
        keep = lax.dynamic_index_in_dim(split, c, 0, keepdims=False)
        give = lax.dynamic_index_in_dim(split, 1 - c, 0, keepdims=False)
        own_gradient = keep + lax.ppermute(give, "sc", swap)
        own = shrink_soft(own, own_gradient, own_cutoff, own_active)
        if sweep + 1 < ITERS:
            own_bf = own.astype(jnp.bfloat16)
            other_bf = lax.ppermute(own_bf, "sc", swap)
            zero = jnp.int32(0)
            weight_bf = lax.dynamic_update_slice(weight_bf, own_bf, (start, zero, zero))
            weight_bf = lax.dynamic_update_slice(
                weight_bf, other_bf, ((1 - c) * share, zero, zero)
            )
    other_half = lax.ppermute(own, "sx", swap)
    mine = jnp.where(
        x == 0,
        jnp.concatenate([own, other_half], axis=1),
        jnp.concatenate([other_half, own], axis=1),
    )
    other_entries = lax.ppermute(mine, "sc", swap)
    return jnp.where(
        c == 0,
        jnp.concatenate([mine, other_entries], axis=0),
        jnp.concatenate([other_entries, mine], axis=0),
    )


def solution(mesh):
    snp_size, samp_size = mesh.devices.shape
    devices = mesh.devices.reshape(snp_size, 2, samp_size // 2)
    mesh = jax.sharding.Mesh(devices, ("snp", "sx", "sc"))
    samp = ("sx", "sc")
    in_specs = (
        P(samp, "snp"),
        P("snp", samp),
        P("snp", None, None),
        P("snp", None),
        P("snp"),
        P(),
        P(),
    )
    out_specs = P("snp", None, None)
    return jax.shard_map(
        per_device, mesh=mesh, in_specs=in_specs, out_specs=out_specs, check_vma=False
    )
```
